256 devices in a mesh: req: 64 (over x, y_lo, z), tp: 4 (over y_hi, core).
Axes of the slice: x: 4, y: 4 (y_hi: 2, y_lo: 2; y = y_hi * 2 + y_lo), z: 8, core: 2. Of those that a mesh axis runs over, the one named last changes fastest.
Arguments:
- hidden_in: bfloat16 [8192, 2048], P('req')
- attn_gain: float32 [2048], replicated, may hold values from 0.1 to 1.9
- w_query: bfloat16 [2048, 2048], P(None, 'tp'), may hold values from -0.125 to 0.125
- w_keyval: bfloat16 [2048, 4, 256], P(None, 'tp'), may hold values from -0.125 to 0.125
- w_out: bfloat16 [2048, 2048], P('tp'), may hold values from -0.125 to 0.125
- moe_gain: float32 [2048], replicated, may hold values from 0.1 to 1.9
- w_gate_up: bfloat16 [64, 2, 2048, 1408], P('req', None, None, 'tp'), may hold values from -0.125 to 0.125
- w_down: bfloat16 [64, 1408, 2048], P('req', 'tp'), may hold values from -0.15625 to 0.15625
- seg_ids: int32 [64, 128], P('req'), may hold values from 0 to 3, never falling along the last dimension, each value on 1 to 64 neighbouring positions
- cached_len: int32 [64], P('req'), may hold values from 2048 to 4096, as said below
- page_table: int32 [64, 32], P('req'), may hold values from 0 to 1023, as said below
- cache_pool: bfloat16 [1024, 4, 128, 256], P('req', 'tp')
- expert_ids: int32 [8192, 6], P('req'), may hold values from 0 to 63, all different within a row; in each aligned block of 128 rows (0 to 127, 128 to 255, ...) at most 16 rows name the same one
- expert_weights: float32 [8192, 6], P('req'), may hold values from 0.05 to 0.5
Outputs:
- layer_out: bfloat16 [8192, 2048], P('req')
The draws below stay inside these ranges and needn't reach their ends.
Inputs may be any that keep to these rules, and one draw needn't show every extreme that they name: `seg_ids`: row r holds the prompt numbers of pack r, never falling along the row; each prompt has 1 to 64 tokens, one exactly that many. `cached_len`: some pack has exactly 4096 cached tokens. `page_table`: entry j of row r names the page holding tokens j * 128 to (j + 1) * 128 - 1 of pack r's cached prefix; page p lies on index p // 16 of req. At most 1 entries of one row lie on one owner, and in every row some owner holds exactly 1. Entries past the cached length name pages too. `expert_ids`: each row names 6 different experts. Among the rows of one pack no expert is named more than 16 times, a bound that some block reaches.
All inputs are finite; a program needn't handle non-finite values.
Results may differ from the reference program's by a relative error of at most 0.009.
Values may be sent and summed in bfloat16 or wider, within the bound.
No kernel may reach another device: no remote copies, remote signals or barrier semaphores. Data moves between devices by JAX's collectives and lax.ppermute only.
A program may use at most 128 MiB of HBM per device.

```python
import math
import jax
import jax.numpy as jnp
import numpy as np
from jax import lax

D = 2048
HEADS = 16
KV_HEADS = 4
HD = 128
FF = 1408
TOPK = 6
EXPERTS = 64
TOK_DEV = 128
SEGS = 4
PREF = 32
PAGE = 128
PAGES_DEV = 16
TOKENS = 8192
CAP_E = 16
N_REQ = 64


def draw_hidden_in(key, part):
    base_key, row_key, col_key = jax.random.split(key, 3)
    row_scale = jnp.exp(jax.random.uniform(row_key, (TOKENS, 1), jnp.float32, math.log(0.3), math.log(3.0)))
    col_scale = jnp.exp(jax.random.uniform(col_key, (1, D), jnp.float32, math.log(0.4), math.log(2.5)))
    raw_vals = jax.random.normal(base_key, (TOKENS, D), jnp.float32)
    return jnp.clip(raw_vals * row_scale * col_scale, -16.0, 16.0).astype(jnp.bfloat16)


def draw_cached_len(key, part):
    value_key, pick_key = jax.random.split(key, 2)
    lengths = jax.random.randint(value_key, (N_REQ,), PREF * PAGE // 2, PREF * PAGE + 1)
    chosen = jax.random.randint(pick_key, (), 0, N_REQ)
    return jnp.where(jnp.arange(N_REQ) == chosen, PREF * PAGE, lengths).astype(jnp.int32)


def owner_order(row_key):
    return jax.random.permutation(row_key, N_REQ)


def entry_order(row_key):
    return jax.random.permutation(row_key, PREF)


def draw_page_table(key, part):
    cap_pages = (2 * PREF + N_REQ - 1) // N_REQ
    owner_key, order_key, slot_key = jax.random.split(key, 3)
    owner_perm = jax.vmap(owner_order)(jax.random.split(owner_key, N_REQ))
    entry_perm = jax.vmap(entry_order)(jax.random.split(order_key, N_REQ))
    owners = jnp.take_along_axis(owner_perm, entry_perm // cap_pages, axis=1)
    slot_ids = jax.random.randint(slot_key, (N_REQ, PREF), 0, PAGES_DEV)
    return (owners * PAGES_DEV + slot_ids).astype(jnp.int32)


def draw_cache_pool(key, part):
    shape = (N_REQ * PAGES_DEV, KV_HEADS, PAGE, 2 * HD)
    base_key, scale_key, offset_key = jax.random.split(key, 3)
    dim_scale = jnp.exp(jax.random.uniform(scale_key, (1, KV_HEADS, 1, HD), jnp.float32, math.log(0.75), math.log(6.0)))
    value_offset = jax.random.normal(offset_key, (N_REQ * PAGES_DEV, KV_HEADS, 1, HD), jnp.float32)
    raw_vals = jax.random.normal(base_key, shape, jnp.float32)
    keys_part = raw_vals[..., :HD] * dim_scale
    values_part = 0.8 * raw_vals[..., HD:] + value_offset
    return jnp.concatenate([keys_part, values_part], axis=-1).astype(jnp.bfloat16)


def shard_levels(own_key, extent, shards, least, top_value):
    loudness = 1.0
    for position, parts in shards:
        heights = jax.random.uniform(jax.random.fold_in(jax.random.fold_in(own_key, 6), position), (parts,), jnp.float32, least / len(shards), top_value / len(shards))
        loudness = loudness * jnp.repeat(jnp.exp(heights), extent[position] // parts).reshape((-1,) + (1,) * (len(extent) - 1 - position))
    return loudness


def length_profile(count, total, reach, skew):
    loads = [(1 << 20) // math.isqrt(rank ** skew) + 1 for rank in range(2, count + 1)]
    surplus, given = total - reach - (count - 1), [1] * (count - 1)
    while surplus > 0:
        free = [i for i in range(count - 1) if given[i] < reach]
        mass, left = sum([loads[i] for i in free]), surplus
        for i in free:
            extra = min(reach - given[i], max(1, left * loads[i] // mass), surplus)
            given[i] = given[i] + extra
            surplus = surplus - extra
    return np.array([reach] + given)


def ragged(stream_key, number_of, total, reach, skew):
    if number_of == 2:
        one = jax.random.randint(stream_key, (), max(1, total - reach), min(reach, total - 1) + 1)
        return jnp.stack([one, total - one])
    tallies = jnp.asarray(length_profile(number_of, total, reach, skew), jnp.int32)
    couples = (number_of - 1) // 2
    donor, taker = tallies[1:1 + 2 * couples:2], tallies[2:2 + 2 * couples:2]
    margin = jnp.minimum(donor - 1, reach - taker)
    passed = jax.random.randint(jax.random.fold_in(stream_key, 1), (couples,), 0, 1 << 20) % (margin + 1)
    tallies = tallies.at[1:1 + 2 * couples:2].set(donor - passed).at[2:2 + 2 * couples:2].set(taker + passed)
    return tallies[jax.random.permutation(jax.random.fold_in(stream_key, 2), number_of)]


def deal_out(stream_key, own, number, rows, amount, top, reach, slope):
    sequence = jax.random.permutation(stream_key, amount)
    heavy_load, usual = portions_of(amount, rows * top, reach, slope, True), portions_of(amount, rows * top, reach, slope, False)
    places = jnp.arange(amount)

    def named(tallies, rotation):
        used = int((tallies > 0).sum())
        fixed = max(1, used // 4)
        moved = fixed + (places - fixed + rotation * (used - fixed)) % max(1, amount - fixed)
        return jnp.zeros((amount,), jnp.int32).at[sequence[jnp.where(places < fixed, places, moved)]].set(jnp.asarray(tallies, jnp.int32))

    tallies = jnp.where(number % 4 == 0, named(heavy_load, number // 4), named(usual, number - number // 4 - 1))
    mixed = jax.random.permutation(jax.random.fold_in(own, 3), amount)
    giver, receiver = mixed[0:amount // 2 * 2:2], mixed[1:amount // 2 * 2:2]
    room = jnp.minimum(tallies[giver] - 1, reach - tallies[receiver]) // 2
    room = jnp.where((giver == sequence[0]) | (receiver == sequence[0]) | (tallies[receiver] == 0), 0, jnp.maximum(room, 0))
    moved = jax.random.randint(jax.random.fold_in(own, 4), (amount // 2,), 0, 1 << 20) % (room + 1)
    tallies = tallies.at[giver].add(-moved).at[receiver].add(moved)
    labels = jnp.searchsorted(jnp.cumsum(tallies), jnp.arange(rows * top), side="right").astype(jnp.int32)
    listing = labels.reshape(top, rows).T
    listing = listing[jax.random.permutation(jax.random.fold_in(own, 1), rows)]
    rotation = jax.random.randint(jax.random.fold_in(own, 2), (rows, 1), 0, top)
    return jnp.take_along_axis(listing, (jnp.arange(top)[None, :] + rotation) % top, axis=1)


def portions_of(amount, total, reach, skew, full):
    portions = [(1 << 20) // math.isqrt(standing ** skew) + 1 for standing in range(1, amount + 1)]
    largest = reach if full else min(reach, max(-(-total // amount), total * portions[0] // sum(portions)))
    least = 1 if total - largest >= amount - 1 else 0
    given, rest = [largest] + [least] * (amount - 1), total - largest - least * (amount - 1)
    while rest > 0:
        movable = [i for i in range(1, amount) if given[i] < largest] or [i for i in range(1, amount) if given[i] < reach]
        pool, remaining = sum([portions[i] for i in movable]), rest
        for i in movable:
            more = min(reach - given[i], max(1, remaining * portions[i] // pool), rest)
            given[i] = given[i] + more
            rest = rest - more
    return np.array(given)


def centred(stream_key, shape, deviation, limit, shards=(), held_as=jnp.bfloat16):
    level = shard_levels(stream_key, shape, shards, -0.22, 0.18) if shards else 1.0
    drawn = jax.random.normal(stream_key, shape, jnp.float32) * deviation * level
    return jnp.minimum(jnp.maximum(drawn, -limit), limit).astype(held_as)


def setup_inputs(seed: int = 0) -> dict:
    seeds = jax.random.split(jax.random.key(seed), 15)
    hidden_in = draw_hidden_in(jax.random.fold_in(seeds[14], 71), 0)
    attn_gain = jnp.clip(1.0 + 0.18 * jax.random.normal(seeds[1], (D,), jnp.float32), 0.1, 1.9)
    w_query = centred(seeds[2], (D, HEADS * HD), D ** -0.5, 0.125, ((1, 4),))
    w_keyval = centred(seeds[3], (D, KV_HEADS, 2 * HD), D ** -0.5, 0.125, ((1, 4),))
    w_out = centred(seeds[4], (HEADS * HD, D), (HEADS * HD) ** -0.5, 0.125, ((0, 4),))
    moe_gain = jnp.clip(1.0 + 0.18 * jax.random.normal(seeds[5], (D,), jnp.float32), 0.1, 1.9)
    w_gate_up = centred(seeds[6], (EXPERTS, 2, D, FF), D ** -0.5, 0.125, ((0, 64), (3, 4)))
    w_down = centred(seeds[7], (EXPERTS, FF, D), FF ** -0.5, 0.15625, ((0, 64), (1, 4)))
    seg_ids = jax.vmap(lambda own: jnp.searchsorted(jnp.cumsum(ragged(own, SEGS, TOK_DEV, TOK_DEV // 2, 2)), jnp.arange(TOK_DEV), side="right"))(jax.random.split(seeds[8], N_REQ)).reshape((N_REQ, TOK_DEV)).astype(jnp.int32)
    cached_len = draw_cached_len(jax.random.fold_in(seeds[14], 71), 0)
    page_table = draw_page_table(jax.random.fold_in(seeds[14], 71), 0)
    cache_pool = draw_cache_pool(jax.random.fold_in(seeds[14], 71), 0)
    expert_ids_keys = jax.random.split(jax.random.fold_in(seeds[12], 1), TOKENS // TOK_DEV)
    expert_ids_turns = jax.random.permutation(jax.random.fold_in(seeds[12], 3), TOKENS // TOK_DEV)
    expert_ids = jax.vmap(lambda own, number: deal_out(jax.random.fold_in(seeds[12], 2), own, number, TOK_DEV, EXPERTS, TOPK, CAP_E, 2))(expert_ids_keys, expert_ids_turns).reshape((TOKENS, TOPK))
    expert_weights = jnp.clip(0.05 + 0.45 * jax.random.uniform(seeds[13], (TOKENS, TOPK), jnp.float32) ** shard_levels(seeds[13], (TOKENS, TOPK), ((0, 64),), -0.2, 0.2), 0.05, 0.5)
    return {"hidden_in": hidden_in, "attn_gain": attn_gain, "w_query": w_query, "w_keyval": w_keyval, "w_out": w_out, "moe_gain": moe_gain, "w_gate_up": w_gate_up, "w_down": w_down, "seg_ids": seg_ids, "cached_len": cached_len, "page_table": page_table, "cache_pool": cache_pool, "expert_ids": expert_ids, "expert_weights": expert_weights}


eps = 1e-06
rope_base = 600000.0

def rms_scale(rows_in, gain):
    widened = rows_in.astype(jnp.float32)
    return widened * lax.rsqrt(lax.optimization_barrier(jnp.mean(widened * widened, axis=-1, keepdims=True)) + eps) * gain

def rotate(vectors, angles):
    half_dim = vectors.shape[-1] // 2
    first_half = vectors[..., :half_dim]
    second_half = vectors[..., half_dim:]
    cosine = jnp.cos(angles)[:, None, :]
    sine_vals = jnp.sin(angles)[:, None, :]
    return jnp.concatenate([first_half * cosine - second_half * sine_vals, second_half * cosine + first_half * sine_vals], axis=-1)

def positions(segment_row, cached):
    length = segment_row.shape[0]
    token_index = jnp.arange(length, dtype=jnp.int32)
    begins = jnp.concatenate([jnp.ones((1,), dtype=bool), segment_row[1:] != segment_row[:-1]])
    seg_start = lax.cummax(jnp.where(begins, token_index, 0), axis=0)
    carried = segment_row == segment_row[0]
    place = token_index - seg_start + jnp.where(carried, cached, 0)
    return (place.astype(jnp.int32), carried)

def make_angles(place, head_dim):
    inverse = rope_base ** (-(jnp.arange(head_dim // 2, dtype=jnp.float32) * 2.0 / head_dim))
    return place.astype(jnp.float32)[:, None] * inverse[None, :]

def admit(segment_row, carried, cached, prefix_len):
    length = segment_row.shape[0]
    token_index = jnp.arange(length, dtype=jnp.int32)
    prefix_ok = (jnp.arange(prefix_len, dtype=jnp.int32)[None, :] < cached) & carried[:, None]
    local_ok = (segment_row[:, None] == segment_row[None, :]) & (token_index[None, :] <= token_index[:, None])
    return jnp.concatenate([prefix_ok, local_ok], axis=1)

def attend(queries, all_keys, all_values, admitted):
    scale = 1.0 / math.sqrt(queries.shape[-1])
    scores = jnp.einsum('tkgd,knd->kgtn', queries.astype(jnp.float32), all_keys.astype(jnp.float32)) * scale
    scores = jnp.where(admitted[None, None], scores, -1e+30)
    highest = lax.optimization_barrier(jnp.max(scores, axis=-1, keepdims=True))
    expo = jnp.exp(scores - highest)
    totals = lax.optimization_barrier(jnp.sum(expo, axis=-1, keepdims=True))
    weights = (expo / totals).astype(jnp.bfloat16)
    context = jnp.einsum('kgtn,knd->tkgd', weights.astype(jnp.float32), all_values.astype(jnp.float32))
    return context.astype(jnp.bfloat16)

def reference(hidden_in, attn_gain, w_query, w_keyval, w_out, moe_gain, w_gate_up, w_down, seg_ids, cached_len, page_table, cache_pool, expert_ids, expert_weights):
    normed = rms_scale(hidden_in, attn_gain).astype(jnp.bfloat16)
    place, carried = jax.vmap(positions)(seg_ids, cached_len)
    angles = make_angles(place.reshape(-1), HD)
    queries = jnp.dot(normed, w_query, preferred_element_type=jnp.float32).reshape(TOKENS, HEADS, HD)
    queries = rotate(queries, angles).astype(jnp.bfloat16)
    keyval = jnp.dot(normed, w_keyval.reshape(D, KV_HEADS * 2 * HD), preferred_element_type=jnp.float32).reshape(TOKENS, KV_HEADS, 2 * HD)
    keys_new = rotate(keyval[..., :HD], angles).astype(jnp.bfloat16)
    values_new = keyval[..., HD:].astype(jnp.bfloat16)

    def one_pack(packed):
        pack_queries, pack_keys, pack_values, segment_row, pack_carried, cached, table_row = packed
        pages = cache_pool[table_row]
        prefix = jnp.transpose(pages, (1, 0, 2, 3)).reshape(KV_HEADS, PREF * PAGE, 2 * HD)
        all_keys = jnp.concatenate([prefix[..., :HD], jnp.transpose(pack_keys, (1, 0, 2))], axis=1)
        all_values = jnp.concatenate([prefix[..., HD:], jnp.transpose(pack_values, (1, 0, 2))], axis=1)
        admitted = admit(segment_row, pack_carried, cached, PREF * PAGE)
        grouped = pack_queries.reshape(TOK_DEV, KV_HEADS, HEADS // KV_HEADS, HD)
        return attend(grouped, all_keys, all_values, admitted).reshape(TOK_DEV, HEADS * HD)
    contexts = lax.map(one_pack, (queries.reshape(N_REQ, TOK_DEV, HEADS, HD), keys_new.reshape(N_REQ, TOK_DEV, KV_HEADS, HD), values_new.reshape(N_REQ, TOK_DEV, KV_HEADS, HD), seg_ids, carried, cached_len, page_table))
    context = contexts.reshape(TOKENS, HEADS * HD)
    attention = jnp.dot(context, w_out, preferred_element_type=jnp.float32)
    resid = (hidden_in.astype(jnp.float32) + attention).astype(jnp.bfloat16)
    normed_moe = rms_scale(resid, moe_gain).astype(jnp.bfloat16)
    flat_ids = expert_ids.reshape(N_REQ, TOK_DEV * TOPK)
    onehot = (flat_ids[..., None] == jnp.arange(EXPERTS, dtype=jnp.int32)[None, None, :]).astype(jnp.int32)
    slot_rank = lax.optimization_barrier(jnp.sum((jnp.cumsum(onehot, axis=1) - 1) * onehot, axis=-1)).astype(jnp.int32)
    pack_index = jnp.broadcast_to(jnp.arange(N_REQ, dtype=jnp.int32)[:, None], flat_ids.shape)
    token_of = (jnp.arange(TOK_DEV * TOPK, dtype=jnp.int32)[None, :] // TOPK + pack_index * TOK_DEV).astype(jnp.int32)
    row_table = jnp.zeros((EXPERTS, N_REQ, CAP_E), jnp.int32).at[flat_ids, pack_index, slot_rank].set(token_of)
    weight_table = jnp.zeros((EXPERTS, N_REQ, CAP_E), jnp.float32).at[flat_ids, pack_index, slot_rank].set(expert_weights.reshape(N_REQ, TOK_DEV * TOPK))

    def expert_step(running, inputs):
        gate_up, down_proj, row_ids, slot_weights = inputs
        flat_rows = row_ids.reshape(-1)
        chosen = normed_moe[flat_rows]
        gate_part = jnp.dot(chosen, gate_up[0], preferred_element_type=jnp.float32)
        up_part = jnp.dot(chosen, gate_up[1], preferred_element_type=jnp.float32)
        hidden_act = (jax.nn.silu(gate_part) * up_part).astype(jnp.bfloat16)
        produced = jnp.dot(hidden_act, down_proj, preferred_element_type=jnp.float32).astype(jnp.bfloat16)
        running = running.at[flat_rows].add(slot_weights.reshape(-1)[:, None] * produced.astype(jnp.float32))
        return (running, None)
    moe_out, _ = lax.scan(expert_step, jnp.zeros((TOKENS, D), jnp.float32), (w_gate_up, w_down, row_table, weight_table))
    return (resid.astype(jnp.float32) + moe_out).astype(jnp.bfloat16)
```

```python
import math

import jax
import jax.numpy as jnp
from jax import lax
from jax.sharding import PartitionSpec as P

eps = 1e-06
rope_base = 600000.0


def rms_scale(rows_in, gain):
    widened = rows_in.astype(jnp.float32)
    return widened * lax.rsqrt(jnp.mean(widened * widened, axis=-1, keepdims=True) + eps) * gain


def rotate(vectors, angles):
    half_dim = vectors.shape[-1] // 2
    first_half = vectors[..., :half_dim]
    second_half = vectors[..., half_dim:]
    cosine = jnp.cos(angles)[:, None, :]
    sine_vals = jnp.sin(angles)[:, None, :]
    return jnp.concatenate(
        [
            first_half * cosine - second_half * sine_vals,
            second_half * cosine + first_half * sine_vals,
        ],
        axis=-1,
    )


def positions(segment_row, cached):
    length = segment_row.shape[0]
    token_index = jnp.arange(length, dtype=jnp.int32)
    begins = jnp.concatenate([jnp.ones((1,), dtype=bool), segment_row[1:] != segment_row[:-1]])
    seg_start = lax.cummax(jnp.where(begins, token_index, 0), axis=0)
    carried = segment_row == segment_row[0]
    place = token_index - seg_start + jnp.where(carried, cached, 0)
    return (place, carried)


def make_angles(place, head_dim):
    inverse = rope_base ** (-(jnp.arange(head_dim // 2, dtype=jnp.float32) * 2.0 / head_dim))
    return place.astype(jnp.float32)[:, None] * inverse[None, :]


def admit(segment_row, carried, cached, prefix_len):
    length = segment_row.shape[0]
    token_index = jnp.arange(length, dtype=jnp.int32)
    prefix_ok = (jnp.arange(prefix_len, dtype=jnp.int32)[None, :] < cached) & carried[:, None]
    local_ok = (segment_row[:, None] == segment_row[None, :]) & (
        token_index[None, :] <= token_index[:, None]
    )
    return jnp.concatenate([prefix_ok, local_ok], axis=1)


def attend(queries, all_keys, all_values, admitted):
    scale = 1.0 / math.sqrt(queries.shape[-1])
    scores = (
        jnp.einsum("tkgd,knd->kgtn", queries, all_keys, preferred_element_type=jnp.float32) * scale
    )
    scores = jnp.where(admitted[None, None], scores, -1e30)
    highest = jnp.max(scores, axis=-1, keepdims=True)
    expo = jnp.exp(scores - highest)
    totals = jnp.sum(expo, axis=-1, keepdims=True)
    weights = (expo / totals).astype(jnp.bfloat16)
    context = jnp.einsum("kgtn,knd->tkgd", weights, all_values, preferred_element_type=jnp.float32)
    return context.astype(jnp.bfloat16)


def shards(
    hidden_in,
    attn_gain,
    w_query,
    w_keyval,
    w_out,
    moe_gain,
    w_gate_up,
    w_down,
    seg_ids,
    cached_len,
    page_table,
    cache_pool,
    expert_ids,
    expert_weights,
):
    tok_rows, model_width = hidden_in.shape
    head_dim = w_keyval.shape[2] // 2
    kv_local = w_keyval.shape[1]
    q_local = w_query.shape[1] // head_dim
    group_size = q_local // kv_local
    segment_row = seg_ids[0]
    cached = cached_len[0]
    place, carried = positions(segment_row, cached)
    angles = make_angles(place, head_dim)
    normed = rms_scale(hidden_in, attn_gain).astype(jnp.bfloat16)
    n_req = lax.axis_size("req")
    listed = page_table[0]
    pref_pages = listed.shape[0]
    pages_dev = cache_pool.shape[0]
    page_len = cache_pool.shape[2]
    cap_pages = (2 * pref_pages + n_req - 1) // n_req
    owners = listed // pages_dev
    entry_index = jnp.arange(pref_pages, dtype=jnp.int32)
    earlier = (owners[None, :] == owners[:, None]) & (entry_index[None, :] < entry_index[:, None])
    owner_rank = jnp.sum(earlier.astype(jnp.int32), axis=1)
    page_slot = listed % pages_dev
    cap_index = jnp.arange(cap_pages, dtype=jnp.int32)
    owner_index = jnp.arange(n_req, dtype=jnp.int32)
    wanted = (owners[None, None, :] == owner_index[:, None, None]) & (
        owner_rank[None, None, :] == cap_index[None, :, None]
    )
    request = jnp.sum(jnp.where(wanted, page_slot[None, None, :], 0), axis=2)
    asked_slots = lax.all_to_all(request, "req", split_axis=0, concat_axis=0, tiled=True)
    served = cache_pool[asked_slots.reshape(-1)].reshape(
        n_req, cap_pages, kv_local, page_len, 2 * head_dim
    )
    fetched = lax.all_to_all(served, "req", split_axis=0, concat_axis=0, tiled=True)
    fetched = fetched.reshape(n_req * cap_pages, kv_local, page_len, 2 * head_dim)[
        owners * cap_pages + owner_rank
    ]
    prefix = jnp.transpose(fetched, (1, 0, 2, 3)).reshape(
        kv_local, pref_pages * page_len, 2 * head_dim
    )
    queries = jnp.dot(normed, w_query, preferred_element_type=jnp.float32).reshape(
        tok_rows, q_local, head_dim
    )
    queries = (
        rotate(queries, angles)
        .astype(jnp.bfloat16)
        .reshape(tok_rows, kv_local, group_size, head_dim)
    )
    keyval = jnp.dot(
        normed,
        w_keyval.reshape(model_width, kv_local * 2 * head_dim),
        preferred_element_type=jnp.float32,
    ).reshape(tok_rows, kv_local, 2 * head_dim)
    keys_new = rotate(keyval[..., :head_dim], angles).astype(jnp.bfloat16)
    values_new = keyval[..., head_dim:].astype(jnp.bfloat16)
    all_keys = jnp.concatenate([prefix[..., :head_dim], jnp.transpose(keys_new, (1, 0, 2))], axis=1)
    all_values = jnp.concatenate(
        [prefix[..., head_dim:], jnp.transpose(values_new, (1, 0, 2))], axis=1
    )
    admitted = admit(segment_row, carried, cached, pref_pages * page_len)
    context = attend(queries, all_keys, all_values, admitted).reshape(tok_rows, q_local * head_dim)
    attention = lax.psum(jnp.dot(context, w_out, preferred_element_type=jnp.float32), "tp")
    resid = (hidden_in.astype(jnp.float32) + attention).astype(jnp.bfloat16)
    moe_in = rms_scale(resid, moe_gain).astype(jnp.bfloat16)
    topk = expert_ids.shape[1]
    n_exp = n_req * w_gate_up.shape[0]
    cap_e = 4 * tok_rows * topk // (3 * n_exp)
    flat_ids = expert_ids.reshape(-1)
    onehot = (flat_ids[:, None] == jnp.arange(n_exp, dtype=jnp.int32)[None, :]).astype(jnp.int32)
    slot_rank = jnp.sum((jnp.cumsum(onehot, axis=0) - 1) * onehot, axis=1)
    assign_slot = flat_ids * cap_e + slot_rank
    slot_match = assign_slot[None, :] == jnp.arange(n_exp * cap_e, dtype=jnp.int32)[:, None]
    selector = jnp.any(slot_match.reshape(n_exp * cap_e, tok_rows, topk), axis=2).astype(
        jnp.bfloat16
    )
    n_tp = lax.axis_size("tp")
    tp_me = lax.axis_index("tp")
    cap_q = cap_e // n_tp
    sel_q = lax.dynamic_slice_in_dim(
        selector.reshape(n_exp, cap_e, tok_rows), tp_me * cap_q, cap_q, axis=1
    )
    outgoing = (
        jnp.einsum("ecs,sd->ecd", sel_q, moe_in, preferred_element_type=jnp.float32)
        .astype(jnp.bfloat16)
        .reshape(n_exp, cap_q * model_width)
    )
    expert_q = lax.all_to_all(outgoing, "req", split_axis=0, concat_axis=0, tiled=True)
    expert_in = lax.all_gather(expert_q, "tp", axis=1, tiled=True)
    expert_rows = expert_in.reshape(-1, model_width)
    gate_part = jnp.dot(expert_rows, w_gate_up[0, 0], preferred_element_type=jnp.float32)
    up_part = jnp.dot(expert_rows, w_gate_up[0, 1], preferred_element_type=jnp.float32)
    hidden_act = (jax.nn.silu(gate_part) * up_part).astype(jnp.bfloat16)
    partial = (
        jnp.dot(hidden_act, w_down[0], preferred_element_type=jnp.float32)
        .astype(jnp.bfloat16)
        .reshape(n_req, cap_e * model_width)
    )
    expert_share = lax.psum_scatter(partial, "tp", scatter_dimension=1, tiled=True)
    results_q = lax.all_to_all(expert_share, "req", split_axis=0, concat_axis=0, tiled=True)
    results = lax.all_gather(results_q, "tp", axis=1, tiled=True)
    picked = results.reshape(-1, model_width)[assign_slot].reshape(tok_rows, topk, model_width)
    moe_out = jnp.sum(expert_weights[:, :, None] * picked.astype(jnp.float32), axis=1)
    return (resid.astype(jnp.float32) + moe_out).astype(jnp.bfloat16)


def solution(mesh):
    in_specs = (
        P("req", None),
        P(),
        P(None, "tp"),
        P(None, "tp", None),
        P("tp", None),
        P(),
        P("req", None, None, "tp"),
        P("req", "tp", None),
        P("req", None),
        P("req"),
        P("req", None),
        P("req", "tp", None, None),
        P("req", None),
        P("req", None),
    )
    out_specs = P("req", None)
    return jax.shard_map(shards, mesh=mesh, in_specs=in_specs, out_specs=out_specs, check_vma=False)
```

```python
import math

import jax
import jax.numpy as jnp
from jax import lax
from jax.sharding import PartitionSpec as P

eps = 1e-06
rope_base = 600000.0


def rms_scale(rows_in, gain):
    widened = rows_in.astype(jnp.float32)
    return widened * lax.rsqrt(jnp.mean(widened * widened, axis=-1, keepdims=True) + eps) * gain


def rotate(vectors, angles):
    half_dim = vectors.shape[-1] // 2
    first_half = vectors[..., :half_dim]
    second_half = vectors[..., half_dim:]
    cosine = jnp.cos(angles)[:, None, :]
    sine_vals = jnp.sin(angles)[:, None, :]
    return jnp.concatenate(
        [
            first_half * cosine - second_half * sine_vals,
            second_half * cosine + first_half * sine_vals,
        ],
        axis=-1,
    )


def positions(segment_row, cached):
    length = segment_row.shape[0]
    token_index = jnp.arange(length, dtype=jnp.int32)
    begins = jnp.concatenate([jnp.ones((1,), dtype=bool), segment_row[1:] != segment_row[:-1]])
    seg_start = lax.cummax(jnp.where(begins, token_index, 0), axis=0)
    carried = segment_row == segment_row[0]
    place = token_index - seg_start + jnp.where(carried, cached, 0)
    return (place, carried)


def make_angles(place, head_dim):
    inverse = rope_base ** (-(jnp.arange(head_dim // 2, dtype=jnp.float32) * 2.0 / head_dim))
    return place.astype(jnp.float32)[:, None] * inverse[None, :]


def admit(segment_row, carried, cached, prefix_len):
    length = segment_row.shape[0]
    token_index = jnp.arange(length, dtype=jnp.int32)
    prefix_ok = (jnp.arange(prefix_len, dtype=jnp.int32)[None, :] < cached) & carried[:, None]
    local_ok = (segment_row[:, None] == segment_row[None, :]) & (
        token_index[None, :] <= token_index[:, None]
    )
    return jnp.concatenate([prefix_ok, local_ok], axis=1)


def attend(queries, all_keys, all_values, admitted):
    scale = 1.0 / math.sqrt(queries.shape[-1])
    scores = (
        jnp.einsum("tkgd,knd->kgtn", queries, all_keys, preferred_element_type=jnp.float32) * scale
    )
    scores = jnp.where(admitted[None, None], scores, -1e30)
    highest = jnp.max(scores, axis=-1, keepdims=True)
    expo = jnp.exp(scores - highest)
    totals = jnp.sum(expo, axis=-1, keepdims=True)
    weights = (expo / totals).astype(jnp.bfloat16)
    context = jnp.einsum("kgtn,knd->tkgd", weights, all_values, preferred_element_type=jnp.float32)
    return context.astype(jnp.bfloat16)


def shards(
    hidden_in,
    attn_gain,
    w_query,
    w_keyval,
    w_out,
    moe_gain,
    w_gate_up,
    w_down,
    seg_ids,
    cached_len,
    page_table,
    cache_pool,
    expert_ids,
    expert_weights,
):
    tok_rows, model_width = hidden_in.shape
    head_dim = w_keyval.shape[2] // 2
    kv_local = w_keyval.shape[1]
    q_local = w_query.shape[1] // head_dim
    group_size = q_local // kv_local
    segment_row = seg_ids[0]
    cached = cached_len[0]
    place, carried = positions(segment_row, cached)
    angles = make_angles(place, head_dim)
    normed = rms_scale(hidden_in, attn_gain).astype(jnp.bfloat16)
    n_req = lax.axis_size("req")
    listed = page_table[0]
    pref_pages = listed.shape[0]
    pages_dev = cache_pool.shape[0]
    page_len = cache_pool.shape[2]
    cap_pages = (2 * pref_pages + n_req - 1) // n_req
    owners = listed // pages_dev
    entry_index = jnp.arange(pref_pages, dtype=jnp.int32)
    earlier = (owners[None, :] == owners[:, None]) & (entry_index[None, :] < entry_index[:, None])
    owner_rank = jnp.sum(earlier.astype(jnp.int32), axis=1)
    page_slot = listed % pages_dev
    cap_index = jnp.arange(cap_pages, dtype=jnp.int32)
    owner_index = jnp.arange(n_req, dtype=jnp.int32)
    wanted = (owners[None, None, :] == owner_index[:, None, None]) & (
        owner_rank[None, None, :] == cap_index[None, :, None]
    )
    request = jnp.sum(jnp.where(wanted, page_slot[None, None, :], 0), axis=2)
    asked_slots = lax.all_to_all(request, "req", split_axis=0, concat_axis=0, tiled=True)
    served = cache_pool[asked_slots.reshape(-1)].reshape(
        n_req, cap_pages, kv_local, page_len, 2 * head_dim
    )
    fetched = lax.all_to_all(served, "req", split_axis=0, concat_axis=0, tiled=True)
    fetched = fetched.reshape(n_req * cap_pages, kv_local, page_len, 2 * head_dim)[
        owners * cap_pages + owner_rank
    ]
    prefix = jnp.transpose(fetched, (1, 0, 2, 3)).reshape(
        kv_local, pref_pages * page_len, 2 * head_dim
    )
    queries = jnp.dot(normed, w_query, preferred_element_type=jnp.float32).reshape(
        tok_rows, q_local, head_dim
    )
    queries = (
        rotate(queries, angles)
        .astype(jnp.bfloat16)
        .reshape(tok_rows, kv_local, group_size, head_dim)
    )
    keyval = jnp.dot(
        normed,
        w_keyval.reshape(model_width, kv_local * 2 * head_dim),
        preferred_element_type=jnp.float32,
    ).reshape(tok_rows, kv_local, 2 * head_dim)
    keys_new = rotate(keyval[..., :head_dim], angles).astype(jnp.bfloat16)
    values_new = keyval[..., head_dim:].astype(jnp.bfloat16)
    all_keys = jnp.concatenate([prefix[..., :head_dim], jnp.transpose(keys_new, (1, 0, 2))], axis=1)
    all_values = jnp.concatenate(
        [prefix[..., head_dim:], jnp.transpose(values_new, (1, 0, 2))], axis=1
    )
    admitted = admit(segment_row, carried, cached, pref_pages * page_len)
    context = attend(queries, all_keys, all_values, admitted).reshape(tok_rows, q_local * head_dim)
    n_tp = lax.axis_size("tp")
    tp_me = lax.axis_index("tp")
    quarter = model_width // n_tp
    attn_part = jnp.einsum(
        "tc,cqd->qtd",
        context,
        w_out.reshape(-1, n_tp, quarter),
        preferred_element_type=jnp.float32,
    )
    attn_q = lax.psum_scatter(attn_part, "tp", scatter_dimension=0, tiled=True)[0]
    hidden_q = lax.dynamic_slice_in_dim(hidden_in, tp_me * quarter, quarter, axis=1)
    resid_q = (hidden_q.astype(jnp.float32) + attn_q).astype(jnp.bfloat16)
    resid_wide = resid_q.astype(jnp.float32)
    sq_sum = lax.psum(jnp.sum(resid_wide * resid_wide, axis=-1, keepdims=True), "tp")
    gain_q = lax.dynamic_slice_in_dim(moe_gain, tp_me * quarter, quarter, axis=0)
    moe_in = (resid_wide * lax.rsqrt(sq_sum / model_width + eps) * gain_q).astype(jnp.bfloat16)
    topk = expert_ids.shape[1]
    n_exp = n_req * w_gate_up.shape[0]
    cap_e = 4 * tok_rows * topk // (3 * n_exp)
    flat_ids = expert_ids.reshape(-1)
    onehot = (flat_ids[:, None] == jnp.arange(n_exp, dtype=jnp.int32)[None, :]).astype(jnp.int32)
    slot_rank = jnp.sum((jnp.cumsum(onehot, axis=0) - 1) * onehot, axis=1)
    assign_slot = flat_ids * cap_e + slot_rank
    slot_match = assign_slot[None, :] == jnp.arange(n_exp * cap_e, dtype=jnp.int32)[:, None]
    selector = jnp.any(slot_match.reshape(n_exp * cap_e, tok_rows, topk), axis=2).astype(
        jnp.bfloat16
    )
    outgoing = (
        jnp.dot(selector, moe_in, preferred_element_type=jnp.float32)
        .astype(jnp.bfloat16)
        .reshape(n_exp, cap_e, quarter)
    )
    expert_q = lax.all_to_all(outgoing, "req", split_axis=0, concat_axis=0, tiled=True)
    expert_in = lax.all_gather(expert_q, "tp", axis=0, tiled=False).reshape(n_tp, -1, quarter)
    hidden_units = w_gate_up.shape[3]
    gate_part = jnp.einsum(
        "qnd,qdh->nh",
        expert_in,
        w_gate_up[0, 0].reshape(n_tp, quarter, hidden_units),
        preferred_element_type=jnp.float32,
    )
    up_part = jnp.einsum(
        "qnd,qdh->nh",
        expert_in,
        w_gate_up[0, 1].reshape(n_tp, quarter, hidden_units),
        preferred_element_type=jnp.float32,
    )
    hidden_act = (jax.nn.silu(gate_part) * up_part).astype(jnp.bfloat16)
    partial = jnp.einsum(
        "nh,hqd->qnd",
        hidden_act,
        w_down[0].reshape(hidden_units, n_tp, quarter),
        preferred_element_type=jnp.float32,
    ).astype(jnp.bfloat16)
    expert_share = lax.psum_scatter(partial, "tp", scatter_dimension=0, tiled=True).reshape(
        n_req, cap_e, quarter
    )
    results = lax.all_to_all(expert_share, "req", split_axis=0, concat_axis=0, tiled=True)
    picked = results.reshape(-1, quarter)[assign_slot].reshape(tok_rows, topk, quarter)
    moe_q = jnp.sum(expert_weights[:, :, None] * picked.astype(jnp.float32), axis=1)
    layer_q = (resid_wide + moe_q).astype(jnp.bfloat16)
    return lax.all_gather(layer_q, "tp", axis=1, tiled=True)


def solution(mesh):
    in_specs = (
        P("req", None),
        P(),
        P(None, "tp"),
        P(None, "tp", None),
        P("tp", None),
        P(),
        P("req", None, None, "tp"),
        P("req", "tp", None),
        P("req", None),
        P("req"),
        P("req", None),
        P("req", "tp", None, None),
        P("req", None),
        P("req", None),
    )
    out_specs = P("req", None)
    return jax.shard_map(shards, mesh=mesh, in_specs=in_specs, out_specs=out_specs, check_vma=False)
```

```python
import math

import jax
import jax.numpy as jnp
from jax import lax
from jax.sharding import PartitionSpec as P

eps = 1e-06
rope_base = 600000.0


def rms_scale(rows_in, gain):
    widened = rows_in.astype(jnp.float32)
    return widened * lax.rsqrt(jnp.mean(widened * widened, axis=-1, keepdims=True) + eps) * gain


def rotate(vectors, angles):
    half_dim = vectors.shape[-1] // 2
    first_half = vectors[..., :half_dim]
    second_half = vectors[..., half_dim:]
    cosine = jnp.cos(angles)[:, None, :]
    sine_vals = jnp.sin(angles)[:, None, :]
    return jnp.concatenate(
        [
            first_half * cosine - second_half * sine_vals,
            second_half * cosine + first_half * sine_vals,
        ],
        axis=-1,
    )


def positions(segment_row, cached):
    length = segment_row.shape[0]
    token_index = jnp.arange(length, dtype=jnp.int32)
    begins = jnp.concatenate([jnp.ones((1,), dtype=bool), segment_row[1:] != segment_row[:-1]])
    seg_start = lax.cummax(jnp.where(begins, token_index, 0), axis=0)
    carried = segment_row == segment_row[0]
    place = token_index - seg_start + jnp.where(carried, cached, 0)
    return (place, carried)


def make_angles(place, head_dim):
    inverse = rope_base ** (-(jnp.arange(head_dim // 2, dtype=jnp.float32) * 2.0 / head_dim))
    return place.astype(jnp.float32)[:, None] * inverse[None, :]


def admit(segment_row, carried, cached, prefix_len):
    length = segment_row.shape[0]
    token_index = jnp.arange(length, dtype=jnp.int32)
    prefix_ok = (jnp.arange(prefix_len, dtype=jnp.int32)[None, :] < cached) & carried[:, None]
    local_ok = (segment_row[:, None] == segment_row[None, :]) & (
        token_index[None, :] <= token_index[:, None]
    )
    return jnp.concatenate([prefix_ok, local_ok], axis=1)


def attend(queries, all_keys, all_values, admitted):
    scale = 1.0 / math.sqrt(queries.shape[-1])
    scores = (
        jnp.einsum("tkgd,knd->kgtn", queries, all_keys, preferred_element_type=jnp.float32) * scale
    )
    scores = jnp.where(admitted[None, None], scores, -1e30)
    highest = jnp.max(scores, axis=-1, keepdims=True)
    expo = jnp.exp(scores - highest)
    totals = jnp.sum(expo, axis=-1, keepdims=True)
    weights = (expo / totals).astype(jnp.bfloat16)
    context = jnp.einsum("kgtn,knd->tkgd", weights, all_values, preferred_element_type=jnp.float32)
    return context.astype(jnp.bfloat16)


ON_CHIP = ((0, 1), (1, 0), (2, 3), (3, 2))
CROSS_CHIP = ((0, 2), (2, 0), (1, 3), (3, 1))


def tp_reduce_scatter(parts, wire_dtype):
    tp_me = lax.axis_index("tp")
    core, half = tp_me % 2, tp_me // 2
    grid = parts.reshape((2, 2) + parts.shape[1:])
    keep = lax.dynamic_index_in_dim(grid, core, axis=1, keepdims=False)
    send = lax.dynamic_index_in_dim(grid, 1 - core, axis=1, keepdims=False)
    got = lax.ppermute(send, "tp", ON_CHIP)
    summed = keep.astype(jnp.float32) + got.astype(jnp.float32)
    mine = lax.dynamic_index_in_dim(summed, half, axis=0, keepdims=False)
    other = lax.dynamic_index_in_dim(summed, 1 - half, axis=0, keepdims=False)
    return mine + lax.ppermute(other.astype(wire_dtype), "tp", CROSS_CHIP).astype(jnp.float32)


def tp_sum(value):
    value = value + lax.ppermute(value, "tp", ON_CHIP)
    return value + lax.ppermute(value, "tp", CROSS_CHIP)


def shards(
    hidden_in,
    attn_gain,
    w_query,
    w_keyval,
    w_out,
    moe_gain,
    w_gate_up,
    w_down,
    seg_ids,
    cached_len,
    page_table,
    cache_pool,
    expert_ids,
    expert_weights,
):
    tok_rows, model_width = hidden_in.shape
    head_dim = w_keyval.shape[2] // 2
    kv_local = w_keyval.shape[1]
    q_local = w_query.shape[1] // head_dim
    group_size = q_local // kv_local
    segment_row = seg_ids[0]
    cached = cached_len[0]
    place, carried = positions(segment_row, cached)
    angles = make_angles(place, head_dim)
    normed = rms_scale(hidden_in, attn_gain).astype(jnp.bfloat16)
    n_req = lax.axis_size("req")
    listed = page_table[0]
    pref_pages = listed.shape[0]
    pages_dev = cache_pool.shape[0]
    page_len = cache_pool.shape[2]
    cap_pages = (2 * pref_pages + n_req - 1) // n_req
    owners = listed // pages_dev
    entry_index = jnp.arange(pref_pages, dtype=jnp.int32)
    earlier = (owners[None, :] == owners[:, None]) & (entry_index[None, :] < entry_index[:, None])
    owner_rank = jnp.sum(earlier.astype(jnp.int32), axis=1)
    page_slot = listed % pages_dev
    cap_index = jnp.arange(cap_pages, dtype=jnp.int32)
    owner_index = jnp.arange(n_req, dtype=jnp.int32)
    wanted = (owners[None, None, :] == owner_index[:, None, None]) & (
        owner_rank[None, None, :] == cap_index[None, :, None]
    )
    request = jnp.sum(jnp.where(wanted, page_slot[None, None, :], 0), axis=2)
    asked_slots = lax.all_to_all(request, "req", split_axis=0, concat_axis=0, tiled=True)
    served = cache_pool[asked_slots.reshape(-1)].reshape(
        n_req, cap_pages, kv_local, page_len, 2 * head_dim
    )
    fetched = lax.all_to_all(served, "req", split_axis=0, concat_axis=0, tiled=True)
    fetched = fetched.reshape(n_req * cap_pages, kv_local, page_len, 2 * head_dim)[
        owners * cap_pages + owner_rank
    ]
    prefix = jnp.transpose(fetched, (1, 0, 2, 3)).reshape(
        kv_local, pref_pages * page_len, 2 * head_dim
    )
    queries = jnp.dot(normed, w_query, preferred_element_type=jnp.float32).reshape(
        tok_rows, q_local, head_dim
    )
    queries = (
        rotate(queries, angles)
        .astype(jnp.bfloat16)
        .reshape(tok_rows, kv_local, group_size, head_dim)
    )
    keyval = jnp.dot(
        normed,
        w_keyval.reshape(model_width, kv_local * 2 * head_dim),
        preferred_element_type=jnp.float32,
    ).reshape(tok_rows, kv_local, 2 * head_dim)
    keys_new = rotate(keyval[..., :head_dim], angles).astype(jnp.bfloat16)
    values_new = keyval[..., head_dim:].astype(jnp.bfloat16)
    all_keys = jnp.concatenate([prefix[..., :head_dim], jnp.transpose(keys_new, (1, 0, 2))], axis=1)
    all_values = jnp.concatenate(
        [prefix[..., head_dim:], jnp.transpose(values_new, (1, 0, 2))], axis=1
    )
    admitted = admit(segment_row, carried, cached, pref_pages * page_len)
    context = attend(queries, all_keys, all_values, admitted).reshape(tok_rows, q_local * head_dim)
    n_tp = lax.axis_size("tp")
    tp_me = lax.axis_index("tp")
    quarter = model_width // n_tp
    attn_part = jnp.einsum(
        "tc,cqd->qtd",
        context,
        w_out.reshape(-1, n_tp, quarter),
        preferred_element_type=jnp.float32,
    )
    attn_q = tp_reduce_scatter(attn_part, jnp.float32)
    hidden_q = lax.dynamic_slice_in_dim(hidden_in, tp_me * quarter, quarter, axis=1)
    resid_q = (hidden_q.astype(jnp.float32) + attn_q).astype(jnp.bfloat16)
    resid_wide = resid_q.astype(jnp.float32)
    sq_sum = tp_sum(jnp.sum(resid_wide * resid_wide, axis=-1, keepdims=True))
    gain_q = lax.dynamic_slice_in_dim(moe_gain, tp_me * quarter, quarter, axis=0)
    moe_in = (resid_wide * lax.rsqrt(sq_sum / model_width + eps) * gain_q).astype(jnp.bfloat16)
    topk = expert_ids.shape[1]
    n_exp = n_req * w_gate_up.shape[0]
    cap_e = 4 * tok_rows * topk // (3 * n_exp)
    flat_ids = expert_ids.reshape(-1)
    onehot = (flat_ids[:, None] == jnp.arange(n_exp, dtype=jnp.int32)[None, :]).astype(jnp.int32)
    slot_rank = jnp.sum((jnp.cumsum(onehot, axis=0) - 1) * onehot, axis=1)
    assign_slot = flat_ids * cap_e + slot_rank
    slot_match = assign_slot[None, :] == jnp.arange(n_exp * cap_e, dtype=jnp.int32)[:, None]
    selector = jnp.any(slot_match.reshape(n_exp * cap_e, tok_rows, topk), axis=2).astype(
        jnp.bfloat16
    )
    outgoing = (
        jnp.dot(selector, moe_in, preferred_element_type=jnp.float32)
        .astype(jnp.bfloat16)
        .reshape(n_exp, cap_e, quarter)
    )
    expert_q = lax.all_to_all(outgoing, "req", split_axis=0, concat_axis=0, tiled=True)
    cross_q = lax.ppermute(expert_q, "tp", CROSS_CHIP)
    chip_pair = jnp.stack([expert_q, cross_q])
    partner_pair = lax.ppermute(chip_pair, "tp", ON_CHIP)
    expert_in = jnp.concatenate([chip_pair, partner_pair]).reshape(n_tp, -1, quarter)
    quarter_order = jnp.stack([tp_me, tp_me ^ 2, tp_me ^ 1, tp_me ^ 3])
    hidden_units = w_gate_up.shape[3]
    gate_w = w_gate_up[0, 0].reshape(n_tp, quarter, hidden_units)[quarter_order]
    up_w = w_gate_up[0, 1].reshape(n_tp, quarter, hidden_units)[quarter_order]
    gate_part = jnp.einsum("qnd,qdh->nh", expert_in, gate_w, preferred_element_type=jnp.float32)
    up_part = jnp.einsum("qnd,qdh->nh", expert_in, up_w, preferred_element_type=jnp.float32)
    hidden_act = (jax.nn.silu(gate_part) * up_part).astype(jnp.bfloat16)
    partial = jnp.einsum(
        "nh,hqd->qnd",
        hidden_act,
        w_down[0].reshape(hidden_units, n_tp, quarter),
        preferred_element_type=jnp.float32,
    ).astype(jnp.bfloat16)
    expert_share = (
        tp_reduce_scatter(partial, jnp.bfloat16).astype(jnp.bfloat16).reshape(n_req, cap_e, quarter)
    )
    results = lax.all_to_all(expert_share, "req", split_axis=0, concat_axis=0, tiled=True)
    picked = results.reshape(-1, quarter)[assign_slot].reshape(tok_rows, topk, quarter)
    moe_q = jnp.sum(expert_weights[:, :, None] * picked.astype(jnp.float32), axis=1)
    layer_q = (resid_wide + moe_q).astype(jnp.bfloat16)
    return lax.all_gather(layer_q, "tp", axis=1, tiled=True)


def solution(mesh):
    in_specs = (
        P("req", None),
        P(),
        P(None, "tp"),
        P(None, "tp", None),
        P("tp", None),
        P(),
        P("req", None, None, "tp"),
        P("req", "tp", None),
        P("req", None),
        P("req"),
        P("req", None),
        P("req", "tp", None, None),
        P("req", None),
        P("req", None),
    )
    out_specs = P("req", None)
    return jax.shard_map(shards, mesh=mesh, in_specs=in_specs, out_specs=out_specs, check_vma=False)
```

```python
import math

import jax
import jax.numpy as jnp
from jax import lax
from jax.sharding import PartitionSpec as P

eps = 1e-06
rope_base = 600000.0


def rms_scale(rows_in, gain):
    widened = rows_in.astype(jnp.float32)
    return widened * lax.rsqrt(jnp.mean(widened * widened, axis=-1, keepdims=True) + eps) * gain


def rotate(vectors, angles):
    half_dim = vectors.shape[-1] // 2
    first_half = vectors[..., :half_dim]
    second_half = vectors[..., half_dim:]
    cosine = jnp.cos(angles)[:, None, :]
    sine_vals = jnp.sin(angles)[:, None, :]
    return jnp.concatenate(
        [
            first_half * cosine - second_half * sine_vals,
            second_half * cosine + first_half * sine_vals,
        ],
        axis=-1,
    )


def positions(segment_row, cached):
    length = segment_row.shape[0]
    token_index = jnp.arange(length, dtype=jnp.int32)
    begins = jnp.concatenate([jnp.ones((1,), dtype=bool), segment_row[1:] != segment_row[:-1]])
    seg_start = lax.cummax(jnp.where(begins, token_index, 0), axis=0)
    carried = segment_row == segment_row[0]
    place = token_index - seg_start + jnp.where(carried, cached, 0)
    return (place, carried)


def make_angles(place, head_dim):
    inverse = rope_base ** (-(jnp.arange(head_dim // 2, dtype=jnp.float32) * 2.0 / head_dim))
    return place.astype(jnp.float32)[:, None] * inverse[None, :]


def admit(segment_row, carried, cached, prefix_len):
    length = segment_row.shape[0]
    token_index = jnp.arange(length, dtype=jnp.int32)
    prefix_ok = (jnp.arange(prefix_len, dtype=jnp.int32)[None, :] < cached) & carried[:, None]
    local_ok = (segment_row[:, None] == segment_row[None, :]) & (
        token_index[None, :] <= token_index[:, None]
    )
    return jnp.concatenate([prefix_ok, local_ok], axis=1)


def attend(queries, all_keys, all_values, admitted):
    scale = 1.0 / math.sqrt(queries.shape[-1])
    scores = (
        jnp.einsum("tkgd,knd->kgtn", queries, all_keys, preferred_element_type=jnp.float32) * scale
    )
    scores = jnp.where(admitted[None, None], scores, -1e30)
    highest = jnp.max(scores, axis=-1, keepdims=True)
    expo = jnp.exp(scores - highest)
    totals = jnp.sum(expo, axis=-1, keepdims=True)
    weights = (expo / totals).astype(jnp.bfloat16)
    context = jnp.einsum("kgtn,knd->tkgd", weights, all_values, preferred_element_type=jnp.float32)
    return context.astype(jnp.bfloat16)


ON_CHIP = ((0, 1), (1, 0), (2, 3), (3, 2))
CROSS_CHIP = ((0, 2), (2, 0), (1, 3), (3, 1))


def tp_reduce_scatter(parts, wire_dtype):
    tp_me = lax.axis_index("tp")
    core, half = tp_me % 2, tp_me // 2
    grid = parts.reshape((2, 2) + parts.shape[1:])
    keep = lax.dynamic_index_in_dim(grid, core, axis=1, keepdims=False)
    send = lax.dynamic_index_in_dim(grid, 1 - core, axis=1, keepdims=False)
    got = lax.ppermute(send, "tp", ON_CHIP)
    summed = keep.astype(jnp.float32) + got.astype(jnp.float32)
    mine = lax.dynamic_index_in_dim(summed, half, axis=0, keepdims=False)
    other = lax.dynamic_index_in_dim(summed, 1 - half, axis=0, keepdims=False)
    return mine + lax.ppermute(other.astype(wire_dtype), "tp", CROSS_CHIP).astype(jnp.float32)


def tp_sum(value):
    value = value + lax.ppermute(value, "tp", ON_CHIP)
    return value + lax.ppermute(value, "tp", CROSS_CHIP)


def shards(
    hidden_in,
    attn_gain,
    w_query,
    w_keyval,
    w_out,
    moe_gain,
    w_gate_up,
    w_down,
    seg_ids,
    cached_len,
    page_table,
    cache_pool,
    expert_ids,
    expert_weights,
):
    tok_rows, model_width = hidden_in.shape
    head_dim = w_keyval.shape[2] // 2
    kv_local = w_keyval.shape[1]
    q_local = w_query.shape[1] // head_dim
    group_size = q_local // kv_local
    segment_row = seg_ids[0]
    cached = cached_len[0]
    place, carried = positions(segment_row, cached)
    angles = make_angles(place, head_dim)
    normed = rms_scale(hidden_in, attn_gain).astype(jnp.bfloat16)
    n_req = lax.axis_size("req")
    listed = page_table[0]
    pref_pages = listed.shape[0]
    pages_dev = cache_pool.shape[0]
    page_len = cache_pool.shape[2]
    cap_pages = (2 * pref_pages + n_req - 1) // n_req
    owners = listed // pages_dev
    entry_index = jnp.arange(pref_pages, dtype=jnp.int32)
    earlier = (owners[None, :] == owners[:, None]) & (entry_index[None, :] < entry_index[:, None])
    owner_rank = jnp.sum(earlier.astype(jnp.int32), axis=1)
    page_slot = listed % pages_dev
    cap_index = jnp.arange(cap_pages, dtype=jnp.int32)
    owner_index = jnp.arange(n_req, dtype=jnp.int32)
    wanted = (owners[None, None, :] == owner_index[:, None, None]) & (
        owner_rank[None, None, :] == cap_index[None, :, None]
    )
    request = jnp.sum(jnp.where(wanted, page_slot[None, None, :], 0), axis=2)
    asked_slots = lax.all_to_all(request, "req", split_axis=0, concat_axis=0, tiled=True)
    served = cache_pool[asked_slots.reshape(-1)].reshape(
        n_req, cap_pages, kv_local, page_len, 2 * head_dim
    )
    fetched = lax.all_to_all(served, "req", split_axis=0, concat_axis=0, tiled=True)
    fetched = fetched.reshape(n_req * cap_pages, kv_local, page_len, 2 * head_dim)[
        owners * cap_pages + owner_rank
    ]
    prefix = jnp.transpose(fetched, (1, 0, 2, 3)).reshape(
        kv_local, pref_pages * page_len, 2 * head_dim
    )
    queries = jnp.dot(normed, w_query, preferred_element_type=jnp.float32).reshape(
        tok_rows, q_local, head_dim
    )
    queries = (
        rotate(queries, angles)
        .astype(jnp.bfloat16)
        .reshape(tok_rows, kv_local, group_size, head_dim)
    )
    n_tp = lax.axis_size("tp")
    tp_me = lax.axis_index("tp")
    quarter = model_width // n_tp
    quarter_order = jnp.stack([tp_me, tp_me ^ 2, tp_me ^ 1, tp_me ^ 3])
    hidden_units = w_gate_up.shape[3]
    gate_w = w_gate_up[0, 0].reshape(n_tp, quarter, hidden_units)[quarter_order]
    up_w = w_gate_up[0, 1].reshape(n_tp, quarter, hidden_units)[quarter_order]
    down_w = w_down[0].reshape(hidden_units, n_tp, quarter)
    gate_w, up_w, down_w, queries = lax.optimization_barrier((gate_w, up_w, down_w, queries))
    keyval = jnp.dot(
        normed,
        w_keyval.reshape(model_width, kv_local * 2 * head_dim),
        preferred_element_type=jnp.float32,
    ).reshape(tok_rows, kv_local, 2 * head_dim)
    keys_new = rotate(keyval[..., :head_dim], angles).astype(jnp.bfloat16)
    values_new = keyval[..., head_dim:].astype(jnp.bfloat16)
    all_keys = jnp.concatenate([prefix[..., :head_dim], jnp.transpose(keys_new, (1, 0, 2))], axis=1)
    all_values = jnp.concatenate(
        [prefix[..., head_dim:], jnp.transpose(values_new, (1, 0, 2))], axis=1
    )
    admitted = admit(segment_row, carried, cached, pref_pages * page_len)
    context = attend(queries, all_keys, all_values, admitted).reshape(tok_rows, q_local * head_dim)
    attn_part = jnp.einsum(
        "tc,cqd->qtd",
        context,
        w_out.reshape(-1, n_tp, quarter),
        preferred_element_type=jnp.float32,
    )
    attn_q = tp_reduce_scatter(attn_part, jnp.float32)
    hidden_q = lax.dynamic_slice_in_dim(hidden_in, tp_me * quarter, quarter, axis=1)
    resid_q = (hidden_q.astype(jnp.float32) + attn_q).astype(jnp.bfloat16)
    resid_wide = resid_q.astype(jnp.float32)
    sq_sum = tp_sum(jnp.sum(resid_wide * resid_wide, axis=-1, keepdims=True))
    gain_q = lax.dynamic_slice_in_dim(moe_gain, tp_me * quarter, quarter, axis=0)
    moe_in = (resid_wide * lax.rsqrt(sq_sum / model_width + eps) * gain_q).astype(jnp.bfloat16)
    topk = expert_ids.shape[1]
    n_exp = n_req * w_gate_up.shape[0]
    cap_e = 4 * tok_rows * topk // (3 * n_exp)
    flat_ids = expert_ids.reshape(-1)
    onehot = (flat_ids[:, None] == jnp.arange(n_exp, dtype=jnp.int32)[None, :]).astype(jnp.int32)
    slot_rank = jnp.sum((jnp.cumsum(onehot, axis=0) - 1) * onehot, axis=1)
    assign_slot = flat_ids * cap_e + slot_rank
    slot_match = assign_slot[None, :] == jnp.arange(n_exp * cap_e, dtype=jnp.int32)[:, None]
    selector = jnp.any(slot_match.reshape(n_exp * cap_e, tok_rows, topk), axis=2).astype(
        jnp.bfloat16
    )
    outgoing = (
        jnp.dot(selector, moe_in, preferred_element_type=jnp.float32)
        .astype(jnp.bfloat16)
        .reshape(n_exp, cap_e, quarter)
    )
    expert_q = lax.all_to_all(outgoing, "req", split_axis=0, concat_axis=0, tiled=True)
    cross_q = lax.ppermute(expert_q, "tp", CROSS_CHIP)
    chip_pair = jnp.stack([expert_q, cross_q])
    partner_pair = lax.ppermute(chip_pair, "tp", ON_CHIP)
    expert_in = jnp.concatenate([chip_pair, partner_pair]).reshape(n_tp, -1, quarter)
    gate_part = jnp.einsum("qnd,qdh->nh", expert_in, gate_w, preferred_element_type=jnp.float32)
    up_part = jnp.einsum("qnd,qdh->nh", expert_in, up_w, preferred_element_type=jnp.float32)
    hidden_act = (jax.nn.silu(gate_part) * up_part).astype(jnp.bfloat16)
    partial = jnp.einsum(
        "nh,hqd->qnd",
        hidden_act,
        down_w,
        preferred_element_type=jnp.float32,
    ).astype(jnp.bfloat16)
    expert_share = (
        tp_reduce_scatter(partial, jnp.bfloat16).astype(jnp.bfloat16).reshape(n_req, cap_e, quarter)
    )
    results = lax.all_to_all(expert_share, "req", split_axis=0, concat_axis=0, tiled=True)
    picked = results.reshape(-1, quarter)[assign_slot].reshape(tok_rows, topk, quarter)
    moe_q = jnp.sum(expert_weights[:, :, None] * picked.astype(jnp.float32), axis=1)
    layer_q = (resid_wide + moe_q).astype(jnp.bfloat16)
    return lax.all_gather(layer_q, "tp", axis=1, tiled=True)


def solution(mesh):
    in_specs = (
        P("req", None),
        P(),
        P(None, "tp"),
        P(None, "tp", None),
        P("tp", None),
        P(),
        P("req", None, None, "tp"),
        P("req", "tp", None),
        P("req", None),
        P("req"),
        P("req", None),
        P("req", "tp", None, None),
        P("req", None),
        P("req", None),
    )
    out_specs = P("req", None)
    return jax.shard_map(shards, mesh=mesh, in_specs=in_specs, out_specs=out_specs, check_vma=False)
```

```python
import math

import jax
import jax.numpy as jnp
from jax import lax
from jax.sharding import PartitionSpec as P

eps = 1e-06
rope_base = 600000.0


def rms_scale(rows_in, gain):
    widened = rows_in.astype(jnp.float32)
    return widened * lax.rsqrt(jnp.mean(widened * widened, axis=-1, keepdims=True) + eps) * gain


def rotate(vectors, angles):
    half_dim = vectors.shape[-1] // 2
    first_half = vectors[..., :half_dim]
    second_half = vectors[..., half_dim:]
    cosine = jnp.cos(angles)[:, None, :]
    sine_vals = jnp.sin(angles)[:, None, :]
    return jnp.concatenate(
        [
            first_half * cosine - second_half * sine_vals,
            second_half * cosine + first_half * sine_vals,
        ],
        axis=-1,
    )


def positions(segment_row, cached):
    length = segment_row.shape[0]
    token_index = jnp.arange(length, dtype=jnp.int32)
    begins = jnp.concatenate([jnp.ones((1,), dtype=bool), segment_row[1:] != segment_row[:-1]])
    seg_start = lax.cummax(jnp.where(begins, token_index, 0), axis=0)
    carried = segment_row == segment_row[0]
    place = token_index - seg_start + jnp.where(carried, cached, 0)
    return (place, carried)


def make_angles(place, head_dim):
    inverse = rope_base ** (-(jnp.arange(head_dim // 2, dtype=jnp.float32) * 2.0 / head_dim))
    return place.astype(jnp.float32)[:, None] * inverse[None, :]


def admit(segment_row, carried, cached, prefix_len):
    length = segment_row.shape[0]
    token_index = jnp.arange(length, dtype=jnp.int32)
    prefix_ok = (jnp.arange(prefix_len, dtype=jnp.int32)[None, :] < cached) & carried[:, None]
    local_ok = (segment_row[:, None] == segment_row[None, :]) & (
        token_index[None, :] <= token_index[:, None]
    )
    return jnp.concatenate([prefix_ok, local_ok], axis=1)


def attend(queries, all_keys, all_values, admitted):
    scale = 1.0 / math.sqrt(queries.shape[-1])
    scores = (
        jnp.einsum("tkgd,knd->kgtn", queries, all_keys, preferred_element_type=jnp.float32) * scale
    )
    scores = jnp.where(admitted[None, None], scores, -1e30)
    highest = jnp.max(scores, axis=-1, keepdims=True)
    expo = jnp.exp(scores - highest)
    totals = jnp.sum(expo, axis=-1, keepdims=True)
    weights = (expo / totals).astype(jnp.bfloat16)
    context = jnp.einsum("kgtn,knd->tkgd", weights, all_values, preferred_element_type=jnp.float32)
    return context.astype(jnp.bfloat16)


ON_CHIP = ((0, 1), (1, 0), (2, 3), (3, 2))
CROSS_CHIP = ((0, 2), (2, 0), (1, 3), (3, 1))


def tp_reduce_scatter(parts, wire_dtype):
    got = lax.ppermute(parts[:2], "tp", ON_CHIP)
    summed = parts[2:].astype(jnp.float32) + got.astype(jnp.float32)
    return summed[0] + lax.ppermute(summed[1].astype(wire_dtype), "tp", CROSS_CHIP).astype(
        jnp.float32
    )


def tp_exchange(value):
    return [lax.ppermute(value, "tp", tuple((t, t ^ flip) for t in range(4))) for flip in (1, 2, 3)]


def tp_sum(value):
    near, across, diagonal = tp_exchange(value)
    return (value + near) + (across + diagonal)


def shards(
    hidden_in,
    attn_gain,
    w_query,
    w_keyval,
    w_out,
    moe_gain,
    w_gate_up,
    w_down,
    seg_ids,
    cached_len,
    page_table,
    cache_pool,
    expert_ids,
    expert_weights,
):
    tok_rows, model_width = hidden_in.shape
    head_dim = w_keyval.shape[2] // 2
    kv_local = w_keyval.shape[1]
    q_local = w_query.shape[1] // head_dim
    group_size = q_local // kv_local
    segment_row = seg_ids[0]
    cached = cached_len[0]
    place, carried = positions(segment_row, cached)
    angles = make_angles(place, head_dim)
    normed = rms_scale(hidden_in, attn_gain).astype(jnp.bfloat16)
    n_req = lax.axis_size("req")
    listed = page_table[0]
    pref_pages = listed.shape[0]
    pages_dev = cache_pool.shape[0]
    page_len = cache_pool.shape[2]
    cap_pages = (2 * pref_pages + n_req - 1) // n_req
    owners = listed // pages_dev
    entry_index = jnp.arange(pref_pages, dtype=jnp.int32)
    earlier = (owners[None, :] == owners[:, None]) & (entry_index[None, :] < entry_index[:, None])
    owner_rank = jnp.sum(earlier.astype(jnp.int32), axis=1)
    page_slot = listed % pages_dev
    cap_index = jnp.arange(cap_pages, dtype=jnp.int32)
    owner_index = jnp.arange(n_req, dtype=jnp.int32)
    wanted = (owners[None, None, :] == owner_index[:, None, None]) & (
        owner_rank[None, None, :] == cap_index[None, :, None]
    )
    request = jnp.sum(jnp.where(wanted, page_slot[None, None, :], 0), axis=2)
    asked_slots = lax.all_to_all(request, "req", split_axis=0, concat_axis=0, tiled=True)
    served = cache_pool[asked_slots.reshape(-1)].reshape(
        n_req, cap_pages, kv_local, page_len, 2 * head_dim
    )
    fetched = lax.all_to_all(served, "req", split_axis=0, concat_axis=0, tiled=True)
    fetched = fetched.reshape(n_req * cap_pages, kv_local, page_len, 2 * head_dim)[
        owners * cap_pages + owner_rank
    ]
    prefix = jnp.transpose(fetched, (1, 0, 2, 3)).reshape(
        kv_local, pref_pages * page_len, 2 * head_dim
    )
    queries = jnp.dot(normed, w_query, preferred_element_type=jnp.float32).reshape(
        tok_rows, q_local, head_dim
    )
    queries = (
        rotate(queries, angles)
        .astype(jnp.bfloat16)
        .reshape(tok_rows, kv_local, group_size, head_dim)
    )
    n_tp = lax.axis_size("tp")
    tp_me = lax.axis_index("tp")
    quarter = model_width // n_tp
    quarter_order = jnp.stack([tp_me, tp_me ^ 2, tp_me ^ 1, tp_me ^ 3])
    hidden_units = w_gate_up.shape[3]
    gate_w = w_gate_up[0, 0].reshape(n_tp, quarter, hidden_units)[quarter_order]
    up_w = w_gate_up[0, 1].reshape(n_tp, quarter, hidden_units)[quarter_order]
    scatter_order = jnp.stack([tp_me ^ 1, tp_me ^ 3, tp_me, tp_me ^ 2])
    down_w = w_down[0].reshape(hidden_units, n_tp, quarter)[:, scatter_order]
    out_w = w_out.reshape(-1, n_tp, quarter)[:, scatter_order]
    gate_w, up_w, down_w, out_w, queries = lax.optimization_barrier(
        (gate_w, up_w, down_w, out_w, queries)
    )
    keyval = jnp.dot(
        normed,
        w_keyval.reshape(model_width, kv_local * 2 * head_dim),
        preferred_element_type=jnp.float32,
    ).reshape(tok_rows, kv_local, 2 * head_dim)
    keys_new = rotate(keyval[..., :head_dim], angles).astype(jnp.bfloat16)
    values_new = keyval[..., head_dim:].astype(jnp.bfloat16)
    all_keys = jnp.concatenate([prefix[..., :head_dim], jnp.transpose(keys_new, (1, 0, 2))], axis=1)
    all_values = jnp.concatenate(
        [prefix[..., head_dim:], jnp.transpose(values_new, (1, 0, 2))], axis=1
    )
    admitted = admit(segment_row, carried, cached, pref_pages * page_len)
    context = attend(queries, all_keys, all_values, admitted).reshape(tok_rows, q_local * head_dim)
    attn_part = jnp.einsum(
        "tc,cqd->qtd",
        context,
        out_w,
        preferred_element_type=jnp.float32,
    )
    attn_q = tp_reduce_scatter(attn_part, jnp.float32)
    hidden_q = lax.dynamic_slice_in_dim(hidden_in, tp_me * quarter, quarter, axis=1)
    resid_q = (hidden_q.astype(jnp.float32) + attn_q).astype(jnp.bfloat16)
    resid_wide = resid_q.astype(jnp.float32)
    sq_sum = tp_sum(jnp.sum(resid_wide * resid_wide, axis=-1, keepdims=True))
    gain_q = lax.dynamic_slice_in_dim(moe_gain, tp_me * quarter, quarter, axis=0)
    moe_in = (resid_wide * lax.rsqrt(sq_sum / model_width + eps) * gain_q).astype(jnp.bfloat16)
    topk = expert_ids.shape[1]
    n_exp = n_req * w_gate_up.shape[0]
    cap_e = 4 * tok_rows * topk // (3 * n_exp)
    flat_ids = expert_ids.reshape(-1)
    onehot = (flat_ids[:, None] == jnp.arange(n_exp, dtype=jnp.int32)[None, :]).astype(jnp.int32)
    slot_rank = jnp.sum((jnp.cumsum(onehot, axis=0) - 1) * onehot, axis=1)
    assign_slot = flat_ids * cap_e + slot_rank
    slot_match = assign_slot[None, :] == jnp.arange(n_exp * cap_e, dtype=jnp.int32)[:, None]
    selector = jnp.any(slot_match.reshape(n_exp * cap_e, tok_rows, topk), axis=2).astype(
        jnp.bfloat16
    )
    outgoing = (
        jnp.dot(selector, moe_in, preferred_element_type=jnp.float32)
        .astype(jnp.bfloat16)
        .reshape(n_exp, cap_e, quarter)
    )
    expert_q = lax.all_to_all(outgoing, "req", split_axis=0, concat_axis=0, tiled=True)
    cross_q = lax.ppermute(expert_q, "tp", CROSS_CHIP)
    chip_pair = jnp.stack([expert_q, cross_q])
    partner_pair = lax.ppermute(chip_pair, "tp", ON_CHIP)
    expert_in = jnp.concatenate([chip_pair, partner_pair]).reshape(n_tp, -1, quarter)
    gate_part = jnp.einsum("qnd,qdh->nh", expert_in, gate_w, preferred_element_type=jnp.float32)
    up_part = jnp.einsum("qnd,qdh->nh", expert_in, up_w, preferred_element_type=jnp.float32)
    hidden_act = (jax.nn.silu(gate_part) * up_part).astype(jnp.bfloat16)
    partial = jnp.einsum(
        "nh,hqd->qnd",
        hidden_act,
        down_w,
        preferred_element_type=jnp.float32,
    ).astype(jnp.bfloat16)
    expert_share = (
        tp_reduce_scatter(partial, jnp.bfloat16).astype(jnp.bfloat16).reshape(n_req, cap_e, quarter)
    )
    results = lax.all_to_all(expert_share, "req", split_axis=0, concat_axis=0, tiled=True)
    picked = results.reshape(-1, quarter)[assign_slot].reshape(tok_rows, topk, quarter)
    moe_q = jnp.sum(expert_weights[:, :, None] * picked.astype(jnp.float32), axis=1)
    layer_q = (resid_wide + moe_q).astype(jnp.bfloat16)
    return lax.all_gather(layer_q, "tp", axis=1, tiled=True)


def solution(mesh):
    in_specs = (
        P("req", None),
        P(),
        P(None, "tp"),
        P(None, "tp", None),
        P("tp", None),
        P(),
        P("req", None, None, "tp"),
        P("req", "tp", None),
        P("req", None),
        P("req"),
        P("req", None),
        P("req", "tp", None, None),
        P("req", None),
        P("req", None),
    )
    out_specs = P("req", None)
    return jax.shard_map(shards, mesh=mesh, in_specs=in_specs, out_specs=out_specs, check_vma=False)
```

```python
import math

import jax
import jax.numpy as jnp
from jax import lax
from jax.sharding import PartitionSpec as P

eps = 1e-06
rope_base = 600000.0


def rms_scale(rows_in, gain):
    widened = rows_in.astype(jnp.float32)
    return widened * lax.rsqrt(jnp.mean(widened * widened, axis=-1, keepdims=True) + eps) * gain


def rotate(vectors, angles):
    half_dim = vectors.shape[-1] // 2
    first_half = vectors[..., :half_dim]
    second_half = vectors[..., half_dim:]
    cosine = jnp.cos(angles)[:, None, :]
    sine_vals = jnp.sin(angles)[:, None, :]
    return jnp.concatenate(
        [
            first_half * cosine - second_half * sine_vals,
            second_half * cosine + first_half * sine_vals,
        ],
        axis=-1,
    )


def positions(segment_row, cached):
    length = segment_row.shape[0]
    token_index = jnp.arange(length, dtype=jnp.int32)
    begins = jnp.concatenate([jnp.ones((1,), dtype=bool), segment_row[1:] != segment_row[:-1]])
    seg_start = lax.cummax(jnp.where(begins, token_index, 0), axis=0)
    carried = segment_row == segment_row[0]
    place = token_index - seg_start + jnp.where(carried, cached, 0)
    return (place, carried)


def make_angles(place, head_dim):
    inverse = rope_base ** (-(jnp.arange(head_dim // 2, dtype=jnp.float32) * 2.0 / head_dim))
    return place.astype(jnp.float32)[:, None] * inverse[None, :]


def admit(segment_row, carried, cached, prefix_len):
    length = segment_row.shape[0]
    token_index = jnp.arange(length, dtype=jnp.int32)
    prefix_ok = (jnp.arange(prefix_len, dtype=jnp.int32)[None, :] < cached) & carried[:, None]
    local_ok = (segment_row[:, None] == segment_row[None, :]) & (
        token_index[None, :] <= token_index[:, None]
    )
    return jnp.concatenate([prefix_ok, local_ok], axis=1)


def attend(queries, all_keys, all_values, admitted):
    scale = 1.0 / math.sqrt(queries.shape[-1])
    scores = (
        jnp.einsum("tkgd,knd->kgtn", queries, all_keys, preferred_element_type=jnp.float32) * scale
    )
    scores = jnp.where(admitted[None, None], scores, -1e30)
    highest = jnp.max(scores, axis=-1, keepdims=True)
    expo = jnp.exp(scores - highest)
    totals = jnp.sum(expo, axis=-1, keepdims=True)
    weights = (expo / totals).astype(jnp.bfloat16)
    context = jnp.einsum("kgtn,knd->tkgd", weights, all_values, preferred_element_type=jnp.float32)
    return context.astype(jnp.bfloat16)


ON_CHIP = ((0, 1), (1, 0), (2, 3), (3, 2))
CROSS_CHIP = ((0, 2), (2, 0), (1, 3), (3, 1))


def tp_reduce_scatter(parts, wire_dtype):
    got = lax.ppermute(parts[:2], "tp", ON_CHIP)
    summed = parts[2:].astype(jnp.float32) + got.astype(jnp.float32)
    return summed[0] + lax.ppermute(summed[1].astype(wire_dtype), "tp", CROSS_CHIP).astype(
        jnp.float32
    )


def tp_exchange(value):
    return [lax.ppermute(value, "tp", tuple((t, t ^ flip) for t in range(4))) for flip in (1, 2, 3)]


def tp_sum(value):
    near, across, diagonal = tp_exchange(value)
    return (value + near) + (across + diagonal)


def shards(
    hidden_in,
    attn_gain,
    w_query,
    w_keyval,
    w_out,
    moe_gain,
    w_gate_up,
    w_down,
    seg_ids,
    cached_len,
    page_table,
    cache_pool,
    expert_ids,
    expert_weights,
):
    tok_rows, model_width = hidden_in.shape
    head_dim = w_keyval.shape[2] // 2
    kv_local = w_keyval.shape[1]
    q_local = w_query.shape[1] // head_dim
    group_size = q_local // kv_local
    segment_row = seg_ids[0]
    cached = cached_len[0]
    place, carried = positions(segment_row, cached)
    angles = make_angles(place, head_dim)
    normed = rms_scale(hidden_in, attn_gain).astype(jnp.bfloat16)
    n_req = lax.axis_size("req")
    listed = page_table[0]
    pref_pages = listed.shape[0]
    pages_dev = cache_pool.shape[0]
    page_len = cache_pool.shape[2]
    cap_pages = (2 * pref_pages + n_req - 1) // n_req
    owners = listed // pages_dev
    entry_index = jnp.arange(pref_pages, dtype=jnp.int32)
    earlier = (owners[None, :] == owners[:, None]) & (entry_index[None, :] < entry_index[:, None])
    owner_rank = jnp.sum(earlier.astype(jnp.int32), axis=1)
    page_slot = listed % pages_dev
    cap_index = jnp.arange(cap_pages, dtype=jnp.int32)
    owner_index = jnp.arange(n_req, dtype=jnp.int32)
    wanted = (owners[None, None, :] == owner_index[:, None, None]) & (
        owner_rank[None, None, :] == cap_index[None, :, None]
    )
    request = jnp.sum(jnp.where(wanted, page_slot[None, None, :], 0), axis=2)
    asked_slots = lax.all_to_all(request, "req", split_axis=0, concat_axis=0, tiled=True)
    served = cache_pool[asked_slots.reshape(-1)].reshape(
        n_req, cap_pages, kv_local, page_len, 2 * head_dim
    )
    fetched = lax.all_to_all(served, "req", split_axis=0, concat_axis=0, tiled=True)
    fetched = fetched.reshape(n_req * cap_pages, kv_local, page_len, 2 * head_dim)[
        owners * cap_pages + owner_rank
    ]
    prefix = jnp.transpose(fetched, (1, 0, 2, 3)).reshape(
        kv_local, pref_pages * page_len, 2 * head_dim
    )
    queries = jnp.dot(normed, w_query, preferred_element_type=jnp.float32).reshape(
        tok_rows, q_local, head_dim
    )
    queries = (
        rotate(queries, angles)
        .astype(jnp.bfloat16)
        .reshape(tok_rows, kv_local, group_size, head_dim)
    )
    n_tp = lax.axis_size("tp")
    tp_me = lax.axis_index("tp")
    quarter = model_width // n_tp
    core = tp_me % 2
    quarter_order = jnp.stack([core, core + 2, 1 - core, 3 - core])
    hidden_units = w_gate_up.shape[3]
    gate_w = w_gate_up[0, 0].reshape(n_tp, quarter, hidden_units)[quarter_order]
    up_w = w_gate_up[0, 1].reshape(n_tp, quarter, hidden_units)[quarter_order]
    scatter_order = jnp.stack([tp_me ^ 1, tp_me ^ 3, tp_me, tp_me ^ 2])
    plane_order = jnp.stack([1 - core, 3 - core, core, core + 2])
    down_w = w_down[0].reshape(hidden_units, n_tp, quarter)[:, plane_order]
    out_w = w_out.reshape(-1, n_tp, quarter)[:, scatter_order]
    gate_w, up_w, down_w, out_w, queries = lax.optimization_barrier(
        (gate_w, up_w, down_w, out_w, queries)
    )
    keyval = jnp.dot(
        normed,
        w_keyval.reshape(model_width, kv_local * 2 * head_dim),
        preferred_element_type=jnp.float32,
    ).reshape(tok_rows, kv_local, 2 * head_dim)
    keys_new = rotate(keyval[..., :head_dim], angles).astype(jnp.bfloat16)
    values_new = keyval[..., head_dim:].astype(jnp.bfloat16)
    all_keys = jnp.concatenate([prefix[..., :head_dim], jnp.transpose(keys_new, (1, 0, 2))], axis=1)
    all_values = jnp.concatenate(
        [prefix[..., head_dim:], jnp.transpose(values_new, (1, 0, 2))], axis=1
    )
    admitted = admit(segment_row, carried, cached, pref_pages * page_len)
    context = attend(queries, all_keys, all_values, admitted).reshape(tok_rows, q_local * head_dim)
    attn_part = jnp.einsum(
        "tc,cqd->qtd",
        context,
        out_w,
        preferred_element_type=jnp.float32,
    )
    attn_q = tp_reduce_scatter(attn_part, jnp.float32)
    hidden_q = lax.dynamic_slice_in_dim(hidden_in, tp_me * quarter, quarter, axis=1)
    resid_q = (hidden_q.astype(jnp.float32) + attn_q).astype(jnp.bfloat16)
    resid_wide = resid_q.astype(jnp.float32)
    sq_sum = tp_sum(jnp.sum(resid_wide * resid_wide, axis=-1, keepdims=True))
    gain_q = lax.dynamic_slice_in_dim(moe_gain, tp_me * quarter, quarter, axis=0)
    moe_in = (resid_wide * lax.rsqrt(sq_sum / model_width + eps) * gain_q).astype(jnp.bfloat16)
    topk = expert_ids.shape[1]
    n_exp = n_req * w_gate_up.shape[0]
    cap_e = 4 * tok_rows * topk // (3 * n_exp)
    flat_ids = expert_ids.reshape(-1)
    onehot = (flat_ids[:, None] == jnp.arange(n_exp, dtype=jnp.int32)[None, :]).astype(jnp.int32)
    slot_rank = jnp.sum((jnp.cumsum(onehot, axis=0) - 1) * onehot, axis=1)
    assign_slot = flat_ids * cap_e + slot_rank
    slot_match = assign_slot[None, :] == jnp.arange(n_exp * cap_e, dtype=jnp.int32)[:, None]
    selector = jnp.any(slot_match.reshape(n_exp * cap_e, tok_rows, topk), axis=2).astype(
        jnp.bfloat16
    )
    outgoing = (
        jnp.dot(selector, moe_in, preferred_element_type=jnp.float32)
        .astype(jnp.bfloat16)
        .reshape(n_exp, cap_e, quarter)
    )
    same_core = [
        [r * n_tp + half * 2 + c for half in range(n_tp // 2) for r in range(n_req)]
        for c in range(2)
    ]
    expert_q = lax.all_to_all(
        jnp.concatenate([outgoing, outgoing]),
        ("req", "tp"),
        0,
        0,
        axis_index_groups=same_core,
        tiled=True,
    )
    chip_pair = expert_q.reshape(2, n_req, cap_e, quarter)
    partner_pair = lax.ppermute(chip_pair, "tp", ON_CHIP)
    expert_in = jnp.concatenate([chip_pair, partner_pair]).reshape(n_tp, -1, quarter)
    gate_part = jnp.einsum("qnd,qdh->nh", expert_in, gate_w, preferred_element_type=jnp.float32)
    up_part = jnp.einsum("qnd,qdh->nh", expert_in, up_w, preferred_element_type=jnp.float32)
    hidden_act = (jax.nn.silu(gate_part) * up_part).astype(jnp.bfloat16)
    partial = jnp.einsum(
        "nh,hqd->qnd",
        hidden_act,
        down_w,
        preferred_element_type=jnp.float32,
    ).astype(jnp.bfloat16)
    got = lax.ppermute(partial[:2], "tp", ON_CHIP)
    chip_sum = (partial[2:].astype(jnp.float32) + got.astype(jnp.float32)).astype(jnp.bfloat16)
    both_planes = lax.all_to_all(
        chip_sum.reshape(2 * n_req, cap_e, quarter),
        ("req", "tp"),
        0,
        0,
        axis_index_groups=same_core,
        tiled=True,
    ).reshape(2, n_req, cap_e, quarter)
    results = (both_planes[0].astype(jnp.float32) + both_planes[1].astype(jnp.float32)).astype(
        jnp.bfloat16
    )
    picked = results.reshape(-1, quarter)[assign_slot].reshape(tok_rows, topk, quarter)
    moe_q = jnp.sum(expert_weights[:, :, None] * picked.astype(jnp.float32), axis=1)
    layer_q = (resid_wide + moe_q).astype(jnp.bfloat16)
    return lax.all_gather(layer_q, "tp", axis=1, tiled=True)


def solution(mesh):
    in_specs = (
        P("req", None),
        P(),
        P(None, "tp"),
        P(None, "tp", None),
        P("tp", None),
        P(),
        P("req", None, None, "tp"),
        P("req", "tp", None),
        P("req", None),
        P("req"),
        P("req", None),
        P("req", "tp", None, None),
        P("req", None),
        P("req", None),
    )
    out_specs = P("req", None)
    return jax.shard_map(shards, mesh=mesh, in_specs=in_specs, out_specs=out_specs, check_vma=False)
```

```python
import math

import jax
import jax.numpy as jnp
from jax import lax
from jax.sharding import PartitionSpec as P

eps = 1e-06
rope_base = 600000.0


def rms_scale(rows_in, gain):
    widened = rows_in.astype(jnp.float32)
    return widened * lax.rsqrt(jnp.mean(widened * widened, axis=-1, keepdims=True) + eps) * gain


def rotate(vectors, angles):
    half_dim = vectors.shape[-1] // 2
    first_half = vectors[..., :half_dim]
    second_half = vectors[..., half_dim:]
    cosine = jnp.cos(angles)[:, None, :]
    sine_vals = jnp.sin(angles)[:, None, :]
    return jnp.concatenate(
        [
            first_half * cosine - second_half * sine_vals,
            second_half * cosine + first_half * sine_vals,
        ],
        axis=-1,
    )


def positions(segment_row, cached):
    length = segment_row.shape[0]
    token_index = jnp.arange(length, dtype=jnp.int32)
    begins = jnp.concatenate([jnp.ones((1,), dtype=bool), segment_row[1:] != segment_row[:-1]])
    seg_start = lax.cummax(jnp.where(begins, token_index, 0), axis=0)
    carried = segment_row == segment_row[0]
    place = token_index - seg_start + jnp.where(carried, cached, 0)
    return (place, carried)


def make_angles(place, head_dim):
    inverse = rope_base ** (-(jnp.arange(head_dim // 2, dtype=jnp.float32) * 2.0 / head_dim))
    return place.astype(jnp.float32)[:, None] * inverse[None, :]


def admit(segment_row, carried, cached, prefix_len):
    length = segment_row.shape[0]
    token_index = jnp.arange(length, dtype=jnp.int32)
    prefix_ok = (jnp.arange(prefix_len, dtype=jnp.int32)[None, :] < cached) & carried[:, None]
    local_ok = (segment_row[:, None] == segment_row[None, :]) & (
        token_index[None, :] <= token_index[:, None]
    )
    return jnp.concatenate([prefix_ok, local_ok], axis=1)


def attend(queries, all_keys, all_values, admitted):
    scale = 1.0 / math.sqrt(queries.shape[-1])
    scores = (
        jnp.einsum("tkgd,knd->kgtn", queries, all_keys, preferred_element_type=jnp.float32) * scale
    )
    scores = jnp.where(admitted[None, None], scores, -1e30)
    highest = jnp.max(scores, axis=-1, keepdims=True)
    expo = jnp.exp(scores - highest)
    totals = jnp.sum(expo, axis=-1, keepdims=True)
    weights = (expo / totals).astype(jnp.bfloat16)
    context = jnp.einsum("kgtn,knd->tkgd", weights, all_values, preferred_element_type=jnp.float32)
    return context.astype(jnp.bfloat16)


ON_CHIP = ((0, 1), (1, 0), (2, 3), (3, 2))
CROSS_CHIP = ((0, 2), (2, 0), (1, 3), (3, 1))


def tp_reduce_scatter(parts, wire_dtype):
    got = lax.ppermute(parts[:2], "tp", ON_CHIP)
    summed = parts[2:].astype(jnp.float32) + got.astype(jnp.float32)
    return summed[0] + lax.ppermute(summed[1].astype(wire_dtype), "tp", CROSS_CHIP).astype(
        jnp.float32
    )


def tp_sum(value):
    value = value + lax.ppermute(value, "tp", ON_CHIP)
    return value + lax.ppermute(value, "tp", CROSS_CHIP)


def shards(
    hidden_in,
    attn_gain,
    w_query,
    w_keyval,
    w_out,
    moe_gain,
    w_gate_up,
    w_down,
    seg_ids,
    cached_len,
    page_table,
    cache_pool,
    expert_ids,
    expert_weights,
):
    tok_rows, model_width = hidden_in.shape
    head_dim = w_keyval.shape[2] // 2
    kv_local = w_keyval.shape[1]
    q_local = w_query.shape[1] // head_dim
    group_size = q_local // kv_local
    segment_row = seg_ids[0]
    cached = cached_len[0]
    place, carried = positions(segment_row, cached)
    angles = make_angles(place, head_dim)
    normed = rms_scale(hidden_in, attn_gain).astype(jnp.bfloat16)
    n_req = lax.axis_size("req")
    listed = page_table[0]
    pref_pages = listed.shape[0]
    pages_dev = cache_pool.shape[0]
    page_len = cache_pool.shape[2]
    cap_pages = (2 * pref_pages + n_req - 1) // n_req
    owners = listed // pages_dev
    entry_index = jnp.arange(pref_pages, dtype=jnp.int32)
    earlier = (owners[None, :] == owners[:, None]) & (entry_index[None, :] < entry_index[:, None])
    owner_rank = jnp.sum(earlier.astype(jnp.int32), axis=1)
    page_slot = listed % pages_dev
    cap_index = jnp.arange(cap_pages, dtype=jnp.int32)
    owner_index = jnp.arange(n_req, dtype=jnp.int32)
    wanted = (owners[None, None, :] == owner_index[:, None, None]) & (
        owner_rank[None, None, :] == cap_index[None, :, None]
    )
    request = jnp.sum(jnp.where(wanted, page_slot[None, None, :], 0), axis=2)
    asked_slots = lax.all_to_all(request, "req", split_axis=0, concat_axis=0, tiled=True)
    served = cache_pool[asked_slots.reshape(-1)].reshape(
        n_req, cap_pages, kv_local, page_len, 2 * head_dim
    )
    fetched = lax.all_to_all(served, "req", split_axis=0, concat_axis=0, tiled=True)
    fetched = fetched.reshape(n_req * cap_pages, kv_local, page_len, 2 * head_dim)[
        owners * cap_pages + owner_rank
    ]
    prefix = jnp.transpose(fetched, (1, 0, 2, 3)).reshape(
        kv_local, pref_pages * page_len, 2 * head_dim
    )
    queries = jnp.dot(normed, w_query, preferred_element_type=jnp.float32).reshape(
        tok_rows, q_local, head_dim
    )
    queries = (
        rotate(queries, angles)
        .astype(jnp.bfloat16)
        .reshape(tok_rows, kv_local, group_size, head_dim)
    )
    n_tp = lax.axis_size("tp")
    tp_me = lax.axis_index("tp")
    quarter = model_width // n_tp
    quarter_order = jnp.stack([tp_me, tp_me ^ 2, tp_me ^ 1, tp_me ^ 3])
    hidden_units = w_gate_up.shape[3]
    gate_w = w_gate_up[0, 0].reshape(n_tp, quarter, hidden_units)[quarter_order]
    up_w = w_gate_up[0, 1].reshape(n_tp, quarter, hidden_units)[quarter_order]
    scatter_order = jnp.stack([tp_me ^ 1, tp_me ^ 3, tp_me, tp_me ^ 2])
    down_w = w_down[0].reshape(hidden_units, n_tp, quarter)[:, scatter_order]
    out_w = w_out.reshape(-1, n_tp, quarter)[:, scatter_order]
    topk = expert_ids.shape[1]
    n_exp = n_req * w_gate_up.shape[0]
    cap_e = 4 * tok_rows * topk // (3 * n_exp)
    flat_ids = expert_ids.reshape(-1)
    onehot = (flat_ids[:, None] == jnp.arange(n_exp, dtype=jnp.int32)[None, :]).astype(jnp.int32)
    slot_rank = jnp.sum((jnp.cumsum(onehot, axis=0) - 1) * onehot, axis=1)
    assign_slot = flat_ids * cap_e + slot_rank
    slot_match = assign_slot[None, :] == jnp.arange(n_exp * cap_e, dtype=jnp.int32)[:, None]
    selector = jnp.any(slot_match.reshape(n_exp * cap_e, tok_rows, topk), axis=2).astype(
        jnp.bfloat16
    )
    gate_w, up_w, down_w, out_w, selector, assign_slot, queries = lax.optimization_barrier(
        (gate_w, up_w, down_w, out_w, selector, assign_slot, queries)
    )
    keyval = jnp.dot(
        normed,
        w_keyval.reshape(model_width, kv_local * 2 * head_dim),
        preferred_element_type=jnp.float32,
    ).reshape(tok_rows, kv_local, 2 * head_dim)
    keys_new = rotate(keyval[..., :head_dim], angles).astype(jnp.bfloat16)
    values_new = keyval[..., head_dim:].astype(jnp.bfloat16)
    all_keys = jnp.concatenate([prefix[..., :head_dim], jnp.transpose(keys_new, (1, 0, 2))], axis=1)
    all_values = jnp.concatenate(
        [prefix[..., head_dim:], jnp.transpose(values_new, (1, 0, 2))], axis=1
    )
    admitted = admit(segment_row, carried, cached, pref_pages * page_len)
    context = attend(queries, all_keys, all_values, admitted).reshape(tok_rows, q_local * head_dim)
    attn_part = jnp.einsum(
        "tc,cqd->qtd",
        context,
        out_w,
        preferred_element_type=jnp.float32,
    )
    attn_q = tp_reduce_scatter(attn_part, jnp.float32)
    hidden_q = lax.dynamic_slice_in_dim(hidden_in, tp_me * quarter, quarter, axis=1)
    resid_q = (hidden_q.astype(jnp.float32) + attn_q).astype(jnp.bfloat16)
    resid_wide = resid_q.astype(jnp.float32)
    sq_sum = tp_sum(jnp.sum(resid_wide * resid_wide, axis=-1, keepdims=True))
    gain_q = lax.dynamic_slice_in_dim(moe_gain, tp_me * quarter, quarter, axis=0)
    moe_in = (resid_wide * lax.rsqrt(sq_sum / model_width + eps) * gain_q).astype(jnp.bfloat16)
    outgoing = (
        jnp.dot(selector, moe_in, preferred_element_type=jnp.float32)
        .astype(jnp.bfloat16)
        .reshape(n_exp, cap_e, quarter)
    )
    expert_q = lax.all_to_all(outgoing, "req", split_axis=0, concat_axis=0, tiled=True)
    cross_q = lax.ppermute(expert_q, "tp", CROSS_CHIP)
    chip_pair = jnp.stack([expert_q, cross_q])
    partner_pair = lax.ppermute(chip_pair, "tp", ON_CHIP)
    expert_in = jnp.concatenate([chip_pair, partner_pair]).reshape(n_tp, -1, quarter)
    gate_part = jnp.einsum("qnd,qdh->nh", expert_in, gate_w, preferred_element_type=jnp.float32)
    up_part = jnp.einsum("qnd,qdh->nh", expert_in, up_w, preferred_element_type=jnp.float32)
    hidden_act = (jax.nn.silu(gate_part) * up_part).astype(jnp.bfloat16)
    partial = jnp.einsum(
        "nh,hqd->qnd",
        hidden_act,
        down_w,
        preferred_element_type=jnp.float32,
    ).astype(jnp.bfloat16)
    expert_share = (
        tp_reduce_scatter(partial, jnp.bfloat16).astype(jnp.bfloat16).reshape(n_req, cap_e, quarter)
    )
    results = lax.all_to_all(expert_share, "req", split_axis=0, concat_axis=0, tiled=True)
    picked = results.reshape(-1, quarter)[assign_slot].reshape(tok_rows, topk, quarter)
    moe_q = jnp.sum(expert_weights[:, :, None] * picked.astype(jnp.float32), axis=1)
    layer_q = (resid_wide + moe_q).astype(jnp.bfloat16)
    return lax.all_gather(layer_q, "tp", axis=1, tiled=True)


def solution(mesh):
    in_specs = (
        P("req", None),
        P(),
        P(None, "tp"),
        P(None, "tp", None),
        P("tp", None),
        P(),
        P("req", None, None, "tp"),
        P("req", "tp", None),
        P("req", None),
        P("req"),
        P("req", None),
        P("req", "tp", None, None),
        P("req", None),
        P("req", None),
    )
    out_specs = P("req", None)
    return jax.shard_map(shards, mesh=mesh, in_specs=in_specs, out_specs=out_specs, check_vma=False)
```

```python
import math

import jax
import jax.numpy as jnp
from jax import lax
from jax.sharding import PartitionSpec as P

eps = 1e-06
rope_base = 600000.0


def rms_scale(rows_in, gain):
    widened = rows_in.astype(jnp.float32)
    return widened * lax.rsqrt(jnp.mean(widened * widened, axis=-1, keepdims=True) + eps) * gain


def rotate(vectors, angles):
    half_dim = vectors.shape[-1] // 2
    first_half = vectors[..., :half_dim]
    second_half = vectors[..., half_dim:]
    cosine = jnp.cos(angles)[:, None, :]
    sine_vals = jnp.sin(angles)[:, None, :]
    return jnp.concatenate(
        [
            first_half * cosine - second_half * sine_vals,
            second_half * cosine + first_half * sine_vals,
        ],
        axis=-1,
    )


def positions(segment_row, cached):
    length = segment_row.shape[0]
    token_index = jnp.arange(length, dtype=jnp.int32)
    begins = jnp.concatenate([jnp.ones((1,), dtype=bool), segment_row[1:] != segment_row[:-1]])
    seg_start = lax.cummax(jnp.where(begins, token_index, 0), axis=0)
    carried = segment_row == segment_row[0]
    place = token_index - seg_start + jnp.where(carried, cached, 0)
    return (place, carried)


def make_angles(place, head_dim):
    inverse = rope_base ** (-(jnp.arange(head_dim // 2, dtype=jnp.float32) * 2.0 / head_dim))
    return place.astype(jnp.float32)[:, None] * inverse[None, :]


def admit(segment_row, carried, cached, prefix_len):
    length = segment_row.shape[0]
    token_index = jnp.arange(length, dtype=jnp.int32)
    prefix_ok = (jnp.arange(prefix_len, dtype=jnp.int32)[None, :] < cached) & carried[:, None]
    local_ok = (segment_row[:, None] == segment_row[None, :]) & (
        token_index[None, :] <= token_index[:, None]
    )
    return jnp.concatenate([prefix_ok, local_ok], axis=1)


def attend(queries, all_keys, all_values, admitted):
    scale = 1.0 / math.sqrt(queries.shape[-1])
    scores = (
        jnp.einsum("tkgd,knd->kgtn", queries, all_keys, preferred_element_type=jnp.float32) * scale
    )
    scores = jnp.where(admitted[None, None], scores, -1e30)
    highest = jnp.max(scores, axis=-1, keepdims=True)
    expo = jnp.exp(scores - highest)
    totals = jnp.sum(expo, axis=-1, keepdims=True)
    weights = (expo / totals).astype(jnp.bfloat16)
    context = jnp.einsum("kgtn,knd->tkgd", weights, all_values, preferred_element_type=jnp.float32)
    return context.astype(jnp.bfloat16)


ON_CHIP = ((0, 1), (1, 0), (2, 3), (3, 2))
CROSS_CHIP = ((0, 2), (2, 0), (1, 3), (3, 1))


def tp_reduce_scatter(parts, wire_dtype):
    got = lax.ppermute(parts[:2], "tp", ON_CHIP)
    summed = parts[2:].astype(jnp.float32) + got.astype(jnp.float32)
    return summed[0] + lax.ppermute(summed[1].astype(wire_dtype), "tp", CROSS_CHIP).astype(
        jnp.float32
    )


def tp_sum(value):
    value = value + lax.ppermute(value, "tp", ON_CHIP)
    return value + lax.ppermute(value, "tp", CROSS_CHIP)


def shards(
    hidden_in,
    attn_gain,
    w_query,
    w_keyval,
    w_out,
    moe_gain,
    w_gate_up,
    w_down,
    seg_ids,
    cached_len,
    page_table,
    cache_pool,
    expert_ids,
    expert_weights,
):
    tok_rows, model_width = hidden_in.shape
    head_dim = w_keyval.shape[2] // 2
    kv_local = w_keyval.shape[1]
    q_local = w_query.shape[1] // head_dim
    group_size = q_local // kv_local
    segment_row = seg_ids[0]
    cached = cached_len[0]
    place, carried = positions(segment_row, cached)
    angles = make_angles(place, head_dim)
    normed = rms_scale(hidden_in, attn_gain).astype(jnp.bfloat16)
    n_req = lax.axis_size("req")
    listed = page_table[0]
    pref_pages = listed.shape[0]
    pages_dev = cache_pool.shape[0]
    page_len = cache_pool.shape[2]
    cap_pages = (2 * pref_pages + n_req - 1) // n_req
    owners = listed // pages_dev
    entry_index = jnp.arange(pref_pages, dtype=jnp.int32)
    earlier = (owners[None, :] == owners[:, None]) & (entry_index[None, :] < entry_index[:, None])
    owner_rank = jnp.sum(earlier.astype(jnp.int32), axis=1)
    page_slot = listed % pages_dev
    cap_index = jnp.arange(cap_pages, dtype=jnp.int32)
    owner_index = jnp.arange(n_req, dtype=jnp.int32)
    wanted = (owners[None, None, :] == owner_index[:, None, None]) & (
        owner_rank[None, None, :] == cap_index[None, :, None]
    )
    request = jnp.sum(jnp.where(wanted, page_slot[None, None, :], 0), axis=2)
    asked_slots = lax.all_to_all(request, "req", split_axis=0, concat_axis=0, tiled=True)
    served = cache_pool[asked_slots.reshape(-1)].reshape(
        n_req, cap_pages, kv_local, page_len, 2 * head_dim
    )
    fetched = lax.all_to_all(served, "req", split_axis=0, concat_axis=0, tiled=True)
    fetched = fetched.reshape(n_req * cap_pages, kv_local, page_len, 2 * head_dim)[
        owners * cap_pages + owner_rank
    ]
    prefix = jnp.transpose(fetched, (1, 0, 2, 3)).reshape(
        kv_local, pref_pages * page_len, 2 * head_dim
    )
    queries = jnp.dot(normed, w_query, preferred_element_type=jnp.float32).reshape(
        tok_rows, q_local, head_dim
    )
    queries = (
        rotate(queries, angles)
        .astype(jnp.bfloat16)
        .reshape(tok_rows, kv_local, group_size, head_dim)
    )
    n_tp = lax.axis_size("tp")
    tp_me = lax.axis_index("tp")
    quarter = model_width // n_tp
    quarter_order = jnp.stack([tp_me, tp_me ^ 1, tp_me ^ 2, tp_me ^ 3])
    hidden_units = w_gate_up.shape[3]
    gate_w = w_gate_up[0, 0].reshape(n_tp, quarter, hidden_units)[quarter_order]
    up_w = w_gate_up[0, 1].reshape(n_tp, quarter, hidden_units)[quarter_order]
    scatter_order = jnp.stack([tp_me ^ 1, tp_me ^ 3, tp_me, tp_me ^ 2])
    down_w = w_down[0].reshape(hidden_units, n_tp, quarter)[:, scatter_order]
    out_w = w_out.reshape(-1, n_tp, quarter)[:, scatter_order]
    topk = expert_ids.shape[1]
    n_exp = n_req * w_gate_up.shape[0]
    cap_e = 4 * tok_rows * topk // (3 * n_exp)
    flat_ids = expert_ids.reshape(-1)
    onehot = (flat_ids[:, None] == jnp.arange(n_exp, dtype=jnp.int32)[None, :]).astype(jnp.int32)
    slot_rank = jnp.sum((jnp.cumsum(onehot, axis=0) - 1) * onehot, axis=1)
    assign_slot = flat_ids * cap_e + slot_rank
    slot_match = assign_slot[None, :] == jnp.arange(n_exp * cap_e, dtype=jnp.int32)[:, None]
    selector = jnp.any(slot_match.reshape(n_exp * cap_e, tok_rows, topk), axis=2).astype(
        jnp.bfloat16
    )
    gate_w, up_w, down_w, out_w, selector, assign_slot, queries = lax.optimization_barrier(
        (gate_w, up_w, down_w, out_w, selector, assign_slot, queries)
    )
    keyval = jnp.dot(
        normed,
        w_keyval.reshape(model_width, kv_local * 2 * head_dim),
        preferred_element_type=jnp.float32,
    ).reshape(tok_rows, kv_local, 2 * head_dim)
    keys_new = rotate(keyval[..., :head_dim], angles).astype(jnp.bfloat16)
    values_new = keyval[..., head_dim:].astype(jnp.bfloat16)
    all_keys = jnp.concatenate([prefix[..., :head_dim], jnp.transpose(keys_new, (1, 0, 2))], axis=1)
    all_values = jnp.concatenate(
        [prefix[..., head_dim:], jnp.transpose(values_new, (1, 0, 2))], axis=1
    )
    admitted = admit(segment_row, carried, cached, pref_pages * page_len)
    context = attend(queries, all_keys, all_values, admitted).reshape(tok_rows, q_local * head_dim)
    attn_part = jnp.einsum(
        "tc,cqd->qtd",
        context,
        out_w,
        preferred_element_type=jnp.float32,
    )
    attn_q = tp_reduce_scatter(attn_part, jnp.float32)
    hidden_q = lax.dynamic_slice_in_dim(hidden_in, tp_me * quarter, quarter, axis=1)
    resid_q = (hidden_q.astype(jnp.float32) + attn_q).astype(jnp.bfloat16)
    resid_wide = resid_q.astype(jnp.float32)
    sq_sum = tp_sum(jnp.sum(resid_wide * resid_wide, axis=-1, keepdims=True))
    gain_q = lax.dynamic_slice_in_dim(moe_gain, tp_me * quarter, quarter, axis=0)
    moe_in = (resid_wide * lax.rsqrt(sq_sum / model_width + eps) * gain_q).astype(jnp.bfloat16)
    outgoing = (
        jnp.dot(selector, moe_in, preferred_element_type=jnp.float32)
        .astype(jnp.bfloat16)
        .reshape(n_exp, cap_e, quarter)
    )
    expert_q = lax.all_to_all(outgoing, "req", split_axis=0, concat_axis=0, tiled=True)
    near_q = lax.ppermute(expert_q, "tp", ON_CHIP)
    cross_q = lax.ppermute(expert_q, "tp", CROSS_CHIP)
    far_q = lax.ppermute(cross_q, "tp", ON_CHIP)
    on_chip_in = jnp.stack([expert_q, near_q]).reshape(2, -1, quarter)
    cross_in = jnp.stack([cross_q, far_q]).reshape(2, -1, quarter)

    def contract(weights):
        early = jnp.einsum(
            "qnd,qdh->nh", on_chip_in, weights[:2], preferred_element_type=jnp.float32
        )
        late = jnp.einsum("qnd,qdh->nh", cross_in, weights[2:], preferred_element_type=jnp.float32)
        return early + late

    gate_part = contract(gate_w)
    up_part = contract(up_w)
    hidden_act = (jax.nn.silu(gate_part) * up_part).astype(jnp.bfloat16)
    partial = jnp.einsum(
        "nh,hqd->qnd",
        hidden_act,
        down_w,
        preferred_element_type=jnp.float32,
    ).astype(jnp.bfloat16)
    expert_share = (
        tp_reduce_scatter(partial, jnp.bfloat16).astype(jnp.bfloat16).reshape(n_req, cap_e, quarter)
    )
    results = lax.all_to_all(expert_share, "req", split_axis=0, concat_axis=0, tiled=True)
    picked = results.reshape(-1, quarter)[assign_slot].reshape(tok_rows, topk, quarter)
    moe_q = jnp.sum(expert_weights[:, :, None] * picked.astype(jnp.float32), axis=1)
    layer_q = (resid_wide + moe_q).astype(jnp.bfloat16)
    return lax.all_gather(layer_q, "tp", axis=1, tiled=True)


def solution(mesh):
    in_specs = (
        P("req", None),
        P(),
        P(None, "tp"),
        P(None, "tp", None),
        P("tp", None),
        P(),
        P("req", None, None, "tp"),
        P("req", "tp", None),
        P("req", None),
        P("req"),
        P("req", None),
        P("req", "tp", None, None),
        P("req", None),
        P("req", None),
    )
    out_specs = P("req", None)
    return jax.shard_map(shards, mesh=mesh, in_specs=in_specs, out_specs=out_specs, check_vma=False)
```

```python
import math

import jax
import jax.numpy as jnp
from jax import lax
from jax.sharding import PartitionSpec as P

eps = 1e-06
rope_base = 600000.0


def rms_scale(rows_in, gain):
    widened = rows_in.astype(jnp.float32)
    return widened * lax.rsqrt(jnp.mean(widened * widened, axis=-1, keepdims=True) + eps) * gain


def rotate(vectors, angles):
    half_dim = vectors.shape[-1] // 2
    first_half = vectors[..., :half_dim]
    second_half = vectors[..., half_dim:]
    cosine = jnp.cos(angles)[:, None, :]
    sine_vals = jnp.sin(angles)[:, None, :]
    return jnp.concatenate(
        [
            first_half * cosine - second_half * sine_vals,
            second_half * cosine + first_half * sine_vals,
        ],
        axis=-1,
    )


def positions(segment_row, cached):
    length = segment_row.shape[0]
    token_index = jnp.arange(length, dtype=jnp.int32)
    begins = jnp.concatenate([jnp.ones((1,), dtype=bool), segment_row[1:] != segment_row[:-1]])
    seg_start = lax.cummax(jnp.where(begins, token_index, 0), axis=0)
    carried = segment_row == segment_row[0]
    place = token_index - seg_start + jnp.where(carried, cached, 0)
    return (place, carried)


def make_angles(place, head_dim):
    inverse = rope_base ** (-(jnp.arange(head_dim // 2, dtype=jnp.float32) * 2.0 / head_dim))
    return place.astype(jnp.float32)[:, None] * inverse[None, :]


def admit(segment_row, carried, cached, prefix_len):
    length = segment_row.shape[0]
    token_index = jnp.arange(length, dtype=jnp.int32)
    prefix_ok = (jnp.arange(prefix_len, dtype=jnp.int32)[None, :] < cached) & carried[:, None]
    local_ok = (segment_row[:, None] == segment_row[None, :]) & (
        token_index[None, :] <= token_index[:, None]
    )
    return jnp.concatenate([prefix_ok, local_ok], axis=1)


def attend(queries, all_keys, all_values, admitted):
    scale = 1.0 / math.sqrt(queries.shape[-1])
    scores = (
        jnp.einsum("tkgd,knd->kgtn", queries, all_keys, preferred_element_type=jnp.float32) * scale
    )
    scores = jnp.where(admitted[None, None], scores, -1e30)
    highest = jnp.max(scores, axis=-1, keepdims=True)
    expo = jnp.exp(scores - highest)
    totals = jnp.sum(expo, axis=-1, keepdims=True)
    weights = (expo / totals).astype(jnp.bfloat16)
    context = jnp.einsum("kgtn,knd->tkgd", weights, all_values, preferred_element_type=jnp.float32)
    return context.astype(jnp.bfloat16)


ON_CHIP = ((0, 1), (1, 0), (2, 3), (3, 2))
CROSS_CHIP = ((0, 2), (2, 0), (1, 3), (3, 1))


def tp_reduce_scatter(parts, wire_dtype):
    got = lax.ppermute(parts[:2], "tp", ON_CHIP)
    summed = parts[2:].astype(jnp.float32) + got.astype(jnp.float32)
    return summed[0] + lax.ppermute(summed[1].astype(wire_dtype), "tp", CROSS_CHIP).astype(
        jnp.float32
    )


def tp_sum(value):
    value = value + lax.ppermute(value, "tp", ON_CHIP)
    return value + lax.ppermute(value, "tp", CROSS_CHIP)


def shards(
    hidden_in,
    attn_gain,
    w_query,
    w_keyval,
    w_out,
    moe_gain,
    w_gate_up,
    w_down,
    seg_ids,
    cached_len,
    page_table,
    cache_pool,
    expert_ids,
    expert_weights,
):
    tok_rows, model_width = hidden_in.shape
    head_dim = w_keyval.shape[2] // 2
    kv_local = w_keyval.shape[1]
    q_local = w_query.shape[1] // head_dim
    group_size = q_local // kv_local
    segment_row = seg_ids[0]
    cached = cached_len[0]
    place, carried = positions(segment_row, cached)
    angles = make_angles(place, head_dim)
    normed = rms_scale(hidden_in, attn_gain).astype(jnp.bfloat16)
    n_req = lax.axis_size("req")
    listed = page_table[0]
    pref_pages = listed.shape[0]
    pages_dev = cache_pool.shape[0]
    page_len = cache_pool.shape[2]
    cap_pages = (2 * pref_pages + n_req - 1) // n_req
    owners = listed // pages_dev
    entry_index = jnp.arange(pref_pages, dtype=jnp.int32)
    earlier = (owners[None, :] == owners[:, None]) & (entry_index[None, :] < entry_index[:, None])
    owner_rank = jnp.sum(earlier.astype(jnp.int32), axis=1)
    page_slot = listed % pages_dev
    cap_index = jnp.arange(cap_pages, dtype=jnp.int32)
    owner_index = jnp.arange(n_req, dtype=jnp.int32)
    wanted = (owners[None, None, :] == owner_index[:, None, None]) & (
        owner_rank[None, None, :] == cap_index[None, :, None]
    )
    request = jnp.sum(jnp.where(wanted, page_slot[None, None, :], 0), axis=2)
    asked_slots = lax.all_to_all(request, "req", split_axis=0, concat_axis=0, tiled=True)
    served = cache_pool[asked_slots.reshape(-1)].reshape(
        n_req, cap_pages, kv_local, page_len, 2 * head_dim
    )
    fetched = lax.all_to_all(served, "req", split_axis=0, concat_axis=0, tiled=True)
    fetched = fetched.reshape(n_req * cap_pages, kv_local, page_len, 2 * head_dim)[
        owners * cap_pages + owner_rank
    ]
    prefix = jnp.transpose(fetched, (1, 0, 2, 3)).reshape(
        kv_local, pref_pages * page_len, 2 * head_dim
    )
    queries = jnp.dot(normed, w_query, preferred_element_type=jnp.float32).reshape(
        tok_rows, q_local, head_dim
    )
    queries = (
        rotate(queries, angles)
        .astype(jnp.bfloat16)
        .reshape(tok_rows, kv_local, group_size, head_dim)
    )
    n_tp = lax.axis_size("tp")
    tp_me = lax.axis_index("tp")
    quarter = model_width // n_tp
    quarter_order = jnp.stack([tp_me, tp_me ^ 2, tp_me ^ 1, tp_me ^ 3])
    hidden_units = w_gate_up.shape[3]
    gate_w = w_gate_up[0, 0].reshape(n_tp, quarter, hidden_units)[quarter_order]
    up_w = w_gate_up[0, 1].reshape(n_tp, quarter, hidden_units)[quarter_order]
    scatter_order = jnp.stack([tp_me ^ 1, tp_me ^ 3, tp_me, tp_me ^ 2])
    down_w = w_down[0].reshape(hidden_units, n_tp, quarter)[:, scatter_order]
    out_w = w_out.reshape(-1, n_tp, quarter)[:, scatter_order]
    topk = expert_ids.shape[1]
    n_exp = n_req * w_gate_up.shape[0]
    cap_e = 4 * tok_rows * topk // (3 * n_exp)
    flat_ids = expert_ids.reshape(-1)
    onehot = (flat_ids[:, None] == jnp.arange(n_exp, dtype=jnp.int32)[None, :]).astype(jnp.int32)
    slot_rank = jnp.sum((jnp.cumsum(onehot, axis=0) - 1) * onehot, axis=1)
    assign_slot = flat_ids * cap_e + slot_rank
    slot_match = assign_slot[None, :] == jnp.arange(n_exp * cap_e, dtype=jnp.int32)[:, None]
    selector = jnp.any(slot_match.reshape(n_exp * cap_e, tok_rows, topk), axis=2).astype(
        jnp.bfloat16
    )
    gate_w, up_w, down_w, out_w, selector, assign_slot, queries = lax.optimization_barrier(
        (gate_w, up_w, down_w, out_w, selector, assign_slot, queries)
    )
    keyval = jnp.dot(
        normed,
        w_keyval.reshape(model_width, kv_local * 2 * head_dim),
        preferred_element_type=jnp.float32,
    ).reshape(tok_rows, kv_local, 2 * head_dim)
    keys_new = rotate(keyval[..., :head_dim], angles).astype(jnp.bfloat16)
    values_new = keyval[..., head_dim:].astype(jnp.bfloat16)
    all_keys = jnp.concatenate([prefix[..., :head_dim], jnp.transpose(keys_new, (1, 0, 2))], axis=1)
    all_values = jnp.concatenate(
        [prefix[..., head_dim:], jnp.transpose(values_new, (1, 0, 2))], axis=1
    )
    admitted = admit(segment_row, carried, cached, pref_pages * page_len)
    context = attend(queries, all_keys, all_values, admitted).reshape(tok_rows, q_local * head_dim)
    attn_part = jnp.einsum(
        "tc,cqd->qtd",
        context,
        out_w,
        preferred_element_type=jnp.float32,
    )
    attn_q = tp_reduce_scatter(attn_part, jnp.float32)
    hidden_q = lax.dynamic_slice_in_dim(hidden_in, tp_me * quarter, quarter, axis=1)
    resid_q = (hidden_q.astype(jnp.float32) + attn_q).astype(jnp.bfloat16)
    resid_wide = resid_q.astype(jnp.float32)
    sq_sum = tp_sum(jnp.sum(resid_wide * resid_wide, axis=-1, keepdims=True))
    gain_q = lax.dynamic_slice_in_dim(moe_gain, tp_me * quarter, quarter, axis=0)
    moe_in = (resid_wide * lax.rsqrt(sq_sum / model_width + eps) * gain_q).astype(jnp.bfloat16)
    outgoing = (
        jnp.dot(selector, moe_in, preferred_element_type=jnp.float32)
        .astype(jnp.bfloat16)
        .reshape(n_exp, cap_e, quarter)
    )
    expert_q = lax.all_to_all(outgoing, "req", split_axis=0, concat_axis=0, tiled=True)
    cross_q = lax.ppermute(expert_q, "tp", CROSS_CHIP)
    chip_pair = jnp.stack([expert_q, cross_q])
    partner_pair = lax.ppermute(chip_pair, "tp", ON_CHIP)
    expert_in = jnp.concatenate([chip_pair, partner_pair]).reshape(n_tp, -1, quarter)
    gate_part = jnp.einsum("qnd,qdh->nh", expert_in, gate_w, preferred_element_type=jnp.float32)
    up_part = jnp.einsum("qnd,qdh->nh", expert_in, up_w, preferred_element_type=jnp.float32)
    hidden_act = (jax.nn.silu(gate_part) * up_part).astype(jnp.bfloat16)
    partial = jnp.einsum(
        "nh,hqd->qnd",
        hidden_act,
        down_w,
        preferred_element_type=jnp.float32,
    ).astype(jnp.bfloat16)
    expert_share = (
        tp_reduce_scatter(partial, jnp.bfloat16).astype(jnp.bfloat16).reshape(n_req, cap_e, quarter)
    )
    results = lax.all_to_all(expert_share, "req", split_axis=0, concat_axis=0, tiled=True)
    slot_by_rank = assign_slot.reshape(tok_rows, topk).T.reshape(-1)
    picked = results.reshape(-1, quarter)[slot_by_rank].reshape(topk, tok_rows, quarter)
    moe_q = jnp.sum(expert_weights.T[:, :, None] * picked.astype(jnp.float32), axis=0)
    layer_q = (resid_wide + moe_q).astype(jnp.bfloat16)
    return lax.all_gather(layer_q, "tp", axis=1, tiled=True)


def solution(mesh):
    in_specs = (
        P("req", None),
        P(),
        P(None, "tp"),
        P(None, "tp", None),
        P("tp", None),
        P(),
        P("req", None, None, "tp"),
        P("req", "tp", None),
        P("req", None),
        P("req"),
        P("req", None),
        P("req", "tp", None, None),
        P("req", None),
        P("req", None),
    )
    out_specs = P("req", None)
    return jax.shard_map(shards, mesh=mesh, in_specs=in_specs, out_specs=out_specs, check_vma=False)
```

```python
import math

import jax
import jax.numpy as jnp
from jax import lax
from jax.sharding import PartitionSpec as P

eps = 1e-06
rope_base = 600000.0


def rms_scale(rows_in, gain):
    widened = rows_in.astype(jnp.float32)
    return widened * lax.rsqrt(jnp.mean(widened * widened, axis=-1, keepdims=True) + eps) * gain


def rotate(vectors, angles):
    half_dim = vectors.shape[-1] // 2
    first_half = vectors[..., :half_dim]
    second_half = vectors[..., half_dim:]
    cosine = jnp.cos(angles)[:, None, :]
    sine_vals = jnp.sin(angles)[:, None, :]
    return jnp.concatenate(
        [
            first_half * cosine - second_half * sine_vals,
            second_half * cosine + first_half * sine_vals,
        ],
        axis=-1,
    )


def positions(segment_row, cached):
    length = segment_row.shape[0]
    token_index = jnp.arange(length, dtype=jnp.int32)
    begins = jnp.concatenate([jnp.ones((1,), dtype=bool), segment_row[1:] != segment_row[:-1]])
    seg_start = lax.cummax(jnp.where(begins, token_index, 0), axis=0)
    carried = segment_row == segment_row[0]
    place = token_index - seg_start + jnp.where(carried, cached, 0)
    return (place, carried)


def make_angles(place, head_dim):
    inverse = rope_base ** (-(jnp.arange(head_dim // 2, dtype=jnp.float32) * 2.0 / head_dim))
    return place.astype(jnp.float32)[:, None] * inverse[None, :]


def admit(segment_row, carried, cached, prefix_len):
    length = segment_row.shape[0]
    token_index = jnp.arange(length, dtype=jnp.int32)
    prefix_ok = (jnp.arange(prefix_len, dtype=jnp.int32)[None, :] < cached) & carried[:, None]
    local_ok = (segment_row[:, None] == segment_row[None, :]) & (
        token_index[None, :] <= token_index[:, None]
    )
    return jnp.concatenate([prefix_ok, local_ok], axis=1)


def attend(queries, all_keys, all_values, admitted):
    scale = 1.0 / math.sqrt(queries.shape[-1])
    scores = (
        jnp.einsum("tkgd,knd->kgtn", queries, all_keys, preferred_element_type=jnp.float32) * scale
    )
    scores = jnp.where(admitted[None, None], scores, -1e30)
    highest = jnp.max(scores, axis=-1, keepdims=True)
    expo = jnp.exp(scores - highest)
    totals = jnp.sum(expo, axis=-1, keepdims=True)
    weights = (expo / totals).astype(jnp.bfloat16)
    context = jnp.einsum("kgtn,knd->tkgd", weights, all_values, preferred_element_type=jnp.float32)
    return context.astype(jnp.bfloat16)


ON_CHIP = ((0, 1), (1, 0), (2, 3), (3, 2))
CROSS_CHIP = ((0, 2), (2, 0), (1, 3), (3, 1))


def tp_reduce_scatter(parts, wire_dtype):
    got = lax.ppermute(parts[:2], "tp", ON_CHIP)
    summed = parts[2:].astype(jnp.float32) + got.astype(jnp.float32)
    return summed[0] + lax.ppermute(summed[1].astype(wire_dtype), "tp", CROSS_CHIP).astype(
        jnp.float32
    )


def tp_sum(value):
    value = value + lax.ppermute(value, "tp", ON_CHIP)
    return value + lax.ppermute(value, "tp", CROSS_CHIP)


def shards(
    hidden_in,
    attn_gain,
    w_query,
    w_keyval,
    w_out,
    moe_gain,
    w_gate_up,
    w_down,
    seg_ids,
    cached_len,
    page_table,
    cache_pool,
    expert_ids,
    expert_weights,
):
    tok_rows, model_width = hidden_in.shape
    head_dim = w_keyval.shape[2] // 2
    kv_local = w_keyval.shape[1]
    q_local = w_query.shape[1] // head_dim
    group_size = q_local // kv_local
    segment_row = seg_ids[0]
    cached = cached_len[0]
    place, carried = positions(segment_row, cached)
    angles = make_angles(place, head_dim)
    normed = rms_scale(hidden_in, attn_gain).astype(jnp.bfloat16)
    n_req = lax.axis_size("req")
    listed = page_table[0]
    pref_pages = listed.shape[0]
    pages_dev = cache_pool.shape[0]
    page_len = cache_pool.shape[2]
    cap_pages = (2 * pref_pages + n_req - 1) // n_req
    owners = listed // pages_dev
    entry_index = jnp.arange(pref_pages, dtype=jnp.int32)
    earlier = (owners[None, :] == owners[:, None]) & (entry_index[None, :] < entry_index[:, None])
    owner_rank = jnp.sum(earlier.astype(jnp.int32), axis=1)
    page_slot = listed % pages_dev
    cap_index = jnp.arange(cap_pages, dtype=jnp.int32)
    owner_index = jnp.arange(n_req, dtype=jnp.int32)
    wanted = (owners[None, None, :] == owner_index[:, None, None]) & (
        owner_rank[None, None, :] == cap_index[None, :, None]
    )
    request = jnp.sum(jnp.where(wanted, page_slot[None, None, :], 0), axis=2)
    asked_slots = lax.all_to_all(request, "req", split_axis=0, concat_axis=0, tiled=True)
    served = cache_pool[asked_slots.reshape(-1)].reshape(
        n_req, cap_pages, kv_local, page_len, 2 * head_dim
    )
    fetched = lax.all_to_all(served, "req", split_axis=0, concat_axis=0, tiled=True)
    fetched = fetched.reshape(n_req * cap_pages, kv_local, page_len, 2 * head_dim)[
        owners * cap_pages + owner_rank
    ]
    prefix = jnp.transpose(fetched, (1, 0, 2, 3)).reshape(
        kv_local, pref_pages * page_len, 2 * head_dim
    )
    queries = jnp.dot(normed, w_query, preferred_element_type=jnp.float32).reshape(
        tok_rows, q_local, head_dim
    )
    queries = (
        rotate(queries, angles)
        .astype(jnp.bfloat16)
        .reshape(tok_rows, kv_local, group_size, head_dim)
    )
    n_tp = lax.axis_size("tp")
    tp_me = lax.axis_index("tp")
    quarter = model_width // n_tp
    quarter_order = jnp.stack([tp_me, tp_me ^ 2, tp_me ^ 1, tp_me ^ 3])
    hidden_units = w_gate_up.shape[3]
    gate_w = w_gate_up[0, 0].reshape(n_tp, quarter, hidden_units)[quarter_order]
    up_w = w_gate_up[0, 1].reshape(n_tp, quarter, hidden_units)[quarter_order]
    scatter_order = jnp.stack([tp_me ^ 1, tp_me ^ 3, tp_me, tp_me ^ 2])
    down_w = w_down[0].reshape(hidden_units, n_tp, quarter)[:, scatter_order]
    out_w = w_out.reshape(-1, n_tp, quarter)[:, scatter_order]
    topk = expert_ids.shape[1]
    n_exp = n_req * w_gate_up.shape[0]
    cap_e = 4 * tok_rows * topk // (3 * n_exp)
    flat_ids = expert_ids.reshape(-1)
    onehot = (flat_ids[:, None] == jnp.arange(n_exp, dtype=jnp.int32)[None, :]).astype(jnp.int32)
    slot_rank = jnp.sum((jnp.cumsum(onehot, axis=0) - 1) * onehot, axis=1)
    assign_slot = flat_ids * cap_e + slot_rank
    slot_match = assign_slot[None, :] == jnp.arange(n_exp * cap_e, dtype=jnp.int32)[:, None]
    selector = jnp.any(slot_match.reshape(n_exp * cap_e, tok_rows, topk), axis=2).astype(
        jnp.bfloat16
    )
    gate_w, up_w, down_w, out_w, selector, assign_slot, queries = lax.optimization_barrier(
        (gate_w, up_w, down_w, out_w, selector, assign_slot, queries)
    )
    keyval = jnp.dot(
        normed,
        w_keyval.reshape(model_width, kv_local * 2 * head_dim),
        preferred_element_type=jnp.float32,
    ).reshape(tok_rows, kv_local, 2 * head_dim)
    keys_new = rotate(keyval[..., :head_dim], angles).astype(jnp.bfloat16)
    values_new = keyval[..., head_dim:].astype(jnp.bfloat16)
    all_keys = jnp.concatenate([prefix[..., :head_dim], jnp.transpose(keys_new, (1, 0, 2))], axis=1)
    all_values = jnp.concatenate(
        [prefix[..., head_dim:], jnp.transpose(values_new, (1, 0, 2))], axis=1
    )
    admitted = admit(segment_row, carried, cached, pref_pages * page_len)
    context = attend(queries, all_keys, all_values, admitted).reshape(tok_rows, q_local * head_dim)
    attn_part = jnp.einsum(
        "tc,cqd->qtd",
        context,
        out_w,
        preferred_element_type=jnp.float32,
    )
    attn_q = tp_reduce_scatter(attn_part, jnp.float32)
    hidden_q = lax.dynamic_slice_in_dim(hidden_in, tp_me * quarter, quarter, axis=1)
    resid_q = (hidden_q.astype(jnp.float32) + attn_q).astype(jnp.bfloat16)
    resid_wide = resid_q.astype(jnp.float32)
    sq_sum = tp_sum(jnp.sum(resid_wide * resid_wide, axis=-1, keepdims=True))
    gain_q = lax.dynamic_slice_in_dim(moe_gain, tp_me * quarter, quarter, axis=0)
    moe_in = (resid_wide * lax.rsqrt(sq_sum / model_width + eps) * gain_q).astype(jnp.bfloat16)
    outgoing = (
        jnp.dot(selector, moe_in, preferred_element_type=jnp.float32)
        .astype(jnp.bfloat16)
        .reshape(n_exp, cap_e, quarter)
    )
    expert_q = lax.all_to_all(outgoing, "req", split_axis=0, concat_axis=0, tiled=True)
    cross_q = lax.ppermute(expert_q, "tp", CROSS_CHIP)
    chip_pair = jnp.stack([expert_q, cross_q])
    partner_pair = lax.ppermute(chip_pair, "tp", ON_CHIP)
    expert_in = jnp.concatenate([chip_pair, partner_pair]).reshape(n_tp, -1, quarter)
    gate_part = jnp.einsum("qnd,qdh->nh", expert_in, gate_w, preferred_element_type=jnp.float32)
    up_part = jnp.einsum("qnd,qdh->nh", expert_in, up_w, preferred_element_type=jnp.float32)
    hidden_act = (jax.nn.silu(gate_part) * up_part).astype(jnp.bfloat16)
    partial = jnp.einsum(
        "nh,hqd->nqd",
        hidden_act,
        down_w,
        preferred_element_type=jnp.float32,
    ).astype(jnp.bfloat16)
    got = lax.ppermute(partial[:, :2], "tp", ON_CHIP)
    chip_sum = partial[:, 2:].astype(jnp.float32) + got.astype(jnp.float32)
    from_cross = lax.ppermute(chip_sum[:, 1].astype(jnp.bfloat16), "tp", CROSS_CHIP)
    expert_share = (
        (chip_sum[:, 0] + from_cross.astype(jnp.float32))
        .astype(jnp.bfloat16)
        .reshape(n_req, cap_e, quarter)
    )
    results = lax.all_to_all(expert_share, "req", split_axis=0, concat_axis=0, tiled=True)
    slot_by_rank = assign_slot.reshape(tok_rows, topk).T.reshape(-1)
    picked = results.reshape(-1, quarter)[slot_by_rank].reshape(topk, tok_rows, quarter)
    moe_q = jnp.sum(expert_weights.T[:, :, None] * picked.astype(jnp.float32), axis=0)
    layer_q = (resid_wide + moe_q).astype(jnp.bfloat16)
    return lax.all_gather(layer_q, "tp", axis=1, tiled=True)


def solution(mesh):
    in_specs = (
        P("req", None),
        P(),
        P(None, "tp"),
        P(None, "tp", None),
        P("tp", None),
        P(),
        P("req", None, None, "tp"),
        P("req", "tp", None),
        P("req", None),
        P("req"),
        P("req", None),
        P("req", "tp", None, None),
        P("req", None),
        P("req", None),
    )
    out_specs = P("req", None)
    return jax.shard_map(shards, mesh=mesh, in_specs=in_specs, out_specs=out_specs, check_vma=False)
```

```python
import math

import jax
import jax.numpy as jnp
from jax import lax
from jax.sharding import PartitionSpec as P

eps = 1e-06
rope_base = 600000.0


def rms_scale(rows_in, gain):
    widened = rows_in.astype(jnp.float32)
    return widened * lax.rsqrt(jnp.mean(widened * widened, axis=-1, keepdims=True) + eps) * gain


def rotate(vectors, angles):
    half_dim = vectors.shape[-1] // 2
    first_half = vectors[..., :half_dim]
    second_half = vectors[..., half_dim:]
    cosine = jnp.cos(angles)[:, None, :]
    sine_vals = jnp.sin(angles)[:, None, :]
    return jnp.concatenate(
        [
            first_half * cosine - second_half * sine_vals,
            second_half * cosine + first_half * sine_vals,
        ],
        axis=-1,
    )


def positions(segment_row, cached):
    length = segment_row.shape[0]
    token_index = jnp.arange(length, dtype=jnp.int32)
    begins = jnp.concatenate([jnp.ones((1,), dtype=bool), segment_row[1:] != segment_row[:-1]])
    seg_start = lax.cummax(jnp.where(begins, token_index, 0), axis=0)
    carried = segment_row == segment_row[0]
    place = token_index - seg_start + jnp.where(carried, cached, 0)
    return (place, carried)


def make_angles(place, head_dim):
    inverse = rope_base ** (-(jnp.arange(head_dim // 2, dtype=jnp.float32) * 2.0 / head_dim))
    return place.astype(jnp.float32)[:, None] * inverse[None, :]


def admit(segment_row, carried, cached, prefix_len):
    length = segment_row.shape[0]
    token_index = jnp.arange(length, dtype=jnp.int32)
    prefix_ok = (jnp.arange(prefix_len, dtype=jnp.int32)[None, :] < cached) & carried[:, None]
    local_ok = (segment_row[:, None] == segment_row[None, :]) & (
        token_index[None, :] <= token_index[:, None]
    )
    return jnp.concatenate([prefix_ok, local_ok], axis=1)


def attend(queries, all_keys, all_values, admitted):
    scale = 1.0 / math.sqrt(queries.shape[-1])
    scores = (
        jnp.einsum("tkgd,knd->kgtn", queries, all_keys, preferred_element_type=jnp.float32) * scale
    )
    scores = jnp.where(admitted[None, None], scores, -1e30)
    highest = jnp.max(scores, axis=-1, keepdims=True)
    expo = jnp.exp(scores - highest)
    totals = jnp.sum(expo, axis=-1, keepdims=True)
    weights = (expo / totals).astype(jnp.bfloat16)
    context = jnp.einsum("kgtn,knd->tkgd", weights, all_values, preferred_element_type=jnp.float32)
    return context.astype(jnp.bfloat16)


ON_CHIP = ((0, 1), (1, 0), (2, 3), (3, 2))
CROSS_CHIP = ((0, 2), (2, 0), (1, 3), (3, 1))


def tp_reduce_scatter(parts, wire_dtype):
    got = lax.ppermute(parts[:2], "tp", ON_CHIP)
    summed = parts[2:].astype(jnp.float32) + got.astype(jnp.float32)
    return summed[0] + lax.ppermute(summed[1].astype(wire_dtype), "tp", CROSS_CHIP).astype(
        jnp.float32
    )


def tp_sum(value):
    value = value + lax.ppermute(value, "tp", ON_CHIP)
    return value + lax.ppermute(value, "tp", CROSS_CHIP)


def shards(
    hidden_in,
    attn_gain,
    w_query,
    w_keyval,
    w_out,
    moe_gain,
    w_gate_up,
    w_down,
    seg_ids,
    cached_len,
    page_table,
    cache_pool,
    expert_ids,
    expert_weights,
):
    tok_rows, model_width = hidden_in.shape
    head_dim = w_keyval.shape[2] // 2
    kv_local = w_keyval.shape[1]
    q_local = w_query.shape[1] // head_dim
    group_size = q_local // kv_local
    segment_row = seg_ids[0]
    cached = cached_len[0]
    place, carried = positions(segment_row, cached)
    angles = make_angles(place, head_dim)
    normed = rms_scale(hidden_in, attn_gain).astype(jnp.bfloat16)
    n_req = lax.axis_size("req")
    listed = page_table[0]
    pref_pages = listed.shape[0]
    pages_dev = cache_pool.shape[0]
    page_len = cache_pool.shape[2]
    cap_pages = (2 * pref_pages + n_req - 1) // n_req
    owners = listed // pages_dev
    entry_index = jnp.arange(pref_pages, dtype=jnp.int32)
    earlier = (owners[None, :] == owners[:, None]) & (entry_index[None, :] < entry_index[:, None])
    owner_rank = jnp.sum(earlier.astype(jnp.int32), axis=1)
    page_slot = listed % pages_dev
    cap_index = jnp.arange(cap_pages, dtype=jnp.int32)
    owner_index = jnp.arange(n_req, dtype=jnp.int32)
    wanted = (owners[None, None, :] == owner_index[:, None, None]) & (
        owner_rank[None, None, :] == cap_index[None, :, None]
    )
    request = jnp.sum(jnp.where(wanted, page_slot[None, None, :], 0), axis=2)
    asked_slots = lax.all_to_all(request, "req", split_axis=0, concat_axis=0, tiled=True)
    served = cache_pool[asked_slots.reshape(-1)].reshape(
        n_req, cap_pages, kv_local, page_len, 2 * head_dim
    )
    fetched = lax.all_to_all(served, "req", split_axis=0, concat_axis=0, tiled=True)
    fetched = fetched.reshape(n_req * cap_pages, kv_local, page_len, 2 * head_dim)[
        owners * cap_pages + owner_rank
    ]
    prefix = jnp.transpose(fetched, (1, 0, 2, 3)).reshape(
        kv_local, pref_pages * page_len, 2 * head_dim
    )
    queries = jnp.dot(normed, w_query, preferred_element_type=jnp.float32).reshape(
        tok_rows, q_local, head_dim
    )
    queries = (
        rotate(queries, angles)
        .astype(jnp.bfloat16)
        .reshape(tok_rows, kv_local, group_size, head_dim)
    )
    n_tp = lax.axis_size("tp")
    tp_me = lax.axis_index("tp")
    quarter = model_width // n_tp
    quarter_order = jnp.stack([tp_me, tp_me ^ 2, tp_me ^ 1, tp_me ^ 3])
    hidden_units = w_gate_up.shape[3]
    gate_w = w_gate_up[0, 0].reshape(n_tp, quarter, hidden_units)[quarter_order]
    up_w = w_gate_up[0, 1].reshape(n_tp, quarter, hidden_units)[quarter_order]
    scatter_order = jnp.stack([tp_me ^ 1, tp_me ^ 3, tp_me, tp_me ^ 2])
    down_w = w_down[0].reshape(hidden_units, n_tp, quarter)[:, scatter_order]
    out_w = w_out.reshape(-1, n_tp, quarter)[:, scatter_order]
    topk = expert_ids.shape[1]
    n_exp = n_req * w_gate_up.shape[0]
    cap_e = 4 * tok_rows * topk // (3 * n_exp)
    flat_ids = expert_ids.reshape(-1)
    onehot = (flat_ids[:, None] == jnp.arange(n_exp, dtype=jnp.int32)[None, :]).astype(jnp.int32)
    slot_rank = jnp.sum((jnp.cumsum(onehot, axis=0) - 1) * onehot, axis=1)
    assign_slot = flat_ids * cap_e + slot_rank
    slot_match = assign_slot[None, :] == jnp.arange(n_exp * cap_e, dtype=jnp.int32)[:, None]
    selector = jnp.any(slot_match.reshape(n_exp * cap_e, tok_rows, topk), axis=2).astype(
        jnp.bfloat16
    )
    gate_w, up_w, down_w, out_w, selector, assign_slot, queries = lax.optimization_barrier(
        (gate_w, up_w, down_w, out_w, selector, assign_slot, queries)
    )
    keyval = jnp.dot(
        normed,
        w_keyval.reshape(model_width, kv_local * 2 * head_dim),
        preferred_element_type=jnp.float32,
    ).reshape(tok_rows, kv_local, 2 * head_dim)
    keys_new = rotate(keyval[..., :head_dim], angles).astype(jnp.bfloat16)
    values_new = keyval[..., head_dim:].astype(jnp.bfloat16)
    all_keys = jnp.concatenate([prefix[..., :head_dim], jnp.transpose(keys_new, (1, 0, 2))], axis=1)
    all_values = jnp.concatenate(
        [prefix[..., head_dim:], jnp.transpose(values_new, (1, 0, 2))], axis=1
    )
    admitted = admit(segment_row, carried, cached, pref_pages * page_len)
    context = attend(queries, all_keys, all_values, admitted).reshape(tok_rows, q_local * head_dim)
    attn_part = jnp.einsum(
        "tc,cqd->qtd",
        context,
        out_w,
        preferred_element_type=jnp.float32,
    )
    attn_q = tp_reduce_scatter(attn_part, jnp.float32)
    hidden_q = lax.dynamic_slice_in_dim(hidden_in, tp_me * quarter, quarter, axis=1)
    resid_q = (hidden_q.astype(jnp.float32) + attn_q).astype(jnp.bfloat16)
    resid_wide = resid_q.astype(jnp.float32)
    sq_sum = tp_sum(jnp.sum(resid_wide * resid_wide, axis=-1, keepdims=True))
    gain_q = lax.dynamic_slice_in_dim(moe_gain, tp_me * quarter, quarter, axis=0)
    moe_in = (resid_wide * lax.rsqrt(sq_sum / model_width + eps) * gain_q).astype(jnp.bfloat16)
    outgoing = (
        jnp.dot(selector, moe_in, preferred_element_type=jnp.float32)
        .astype(jnp.bfloat16)
        .reshape(n_exp, cap_e, quarter)
    )
    expert_q = lax.all_to_all(outgoing, "req", split_axis=0, concat_axis=0, tiled=True)
    near_q = lax.ppermute(expert_q, "tp", ON_CHIP)
    cross_q = lax.ppermute(expert_q, "tp", CROSS_CHIP)
    far_q = lax.ppermute(cross_q, "tp", ON_CHIP)
    expert_in = jnp.stack([expert_q, cross_q, near_q, far_q]).reshape(n_tp, -1, quarter)
    gate_part = jnp.einsum("qnd,qdh->nh", expert_in, gate_w, preferred_element_type=jnp.float32)
    up_part = jnp.einsum("qnd,qdh->nh", expert_in, up_w, preferred_element_type=jnp.float32)
    hidden_act = (jax.nn.silu(gate_part) * up_part).astype(jnp.bfloat16)
    partial = jnp.einsum(
        "nh,hqd->nqd",
        hidden_act,
        down_w,
        preferred_element_type=jnp.float32,
    ).astype(jnp.bfloat16)
    got = lax.ppermute(partial[:, :2], "tp", ON_CHIP)
    chip_sum = partial[:, 2:].astype(jnp.float32) + got.astype(jnp.float32)
    from_cross = lax.ppermute(chip_sum[:, 1].astype(jnp.bfloat16), "tp", CROSS_CHIP)
    expert_share = (
        (chip_sum[:, 0] + from_cross.astype(jnp.float32))
        .astype(jnp.bfloat16)
        .reshape(n_req, cap_e, quarter)
    )
    results = lax.all_to_all(expert_share, "req", split_axis=0, concat_axis=0, tiled=True)
    slot_by_rank = assign_slot.reshape(tok_rows, topk).T.reshape(-1)
    picked = results.reshape(-1, quarter)[slot_by_rank].reshape(topk, tok_rows, quarter)
    moe_q = jnp.sum(expert_weights.T[:, :, None] * picked.astype(jnp.float32), axis=0)
    layer_q = (resid_wide + moe_q).astype(jnp.bfloat16)
    return lax.all_gather(layer_q, "tp", axis=1, tiled=True)


def solution(mesh):
    in_specs = (
        P("req", None),
        P(),
        P(None, "tp"),
        P(None, "tp", None),
        P("tp", None),
        P(),
        P("req", None, None, "tp"),
        P("req", "tp", None),
        P("req", None),
        P("req"),
        P("req", None),
        P("req", "tp", None, None),
        P("req", None),
        P("req", None),
    )
    out_specs = P("req", None)
    return jax.shard_map(shards, mesh=mesh, in_specs=in_specs, out_specs=out_specs, check_vma=False)
```
